256 devices in a mesh: seq: 128 (over y_hi, x, z, core), tp: 2 (over y_lo).
Axes of the slice: x: 4, y: 4 (y_hi: 2, y_lo: 2; y = y_hi * 2 + y_lo), z: 8, core: 2. Of those that a mesh axis runs over, the one named last changes fastest.
Arguments:
- noisy: bfloat16 [2, 49152, 1024], P(None, 'seq', 'tp'), may hold values from -6 to 6
- levels: int32 [2], replicated, may hold values from 0 to 999, as said below
- pairs: int32 [384, 4], P('seq'), may hold values from 0 to 383, as said below
- w_qkv: bfloat16 [3, 1024, 1024], P(None, None, 'tp'), may hold values from -4 to 4
- w_out: bfloat16 [1024, 1024], P('tp'), may hold values from -0.1875 to 0.1875
- w_up: bfloat16 [1024, 3072], P(None, 'tp'), may hold values from -0.1875 to 0.1875
- w_down: bfloat16 [3072, 1024], P('tp'), may hold values from -0.109375 to 0.109375
Outputs:
- denoised: bfloat16 [2, 49152, 1024], P(None, 'seq', 'tp')
The draws below stay inside these ranges and needn't reach their ends.
Inputs may be any that keep to these rules, and one draw needn't show every extreme that they name: For query block b and section s, pairs[b, s] lies in the group of 3 consecutive blocks numbered g XOR (384 * 128 // (384 * 2 ** (s + 1))), where g = b // 3; at each section the query blocks of one group name each block of that group once. The samples' levels differ from one another; one sample has level 999.
All inputs are finite; a program needn't handle non-finite values.
Results may differ from the reference program's by a relative error of at most 0.017.
Values may be sent and summed in bfloat16 or wider, within the bound.
No kernel may reach another device: no remote copies, remote signals or barrier semaphores. Data moves between devices by JAX's collectives and lax.ppermute only.
A program may use at most 192 MiB of HBM per device.

```python
import math
import jax
import jax.numpy as jnp
from jax import lax

D = 1024
HEADS = 16
FF = 3072
BLOCK = 128
SECTIONS = 4
NLEV = 1000
SAMPLES = 2
TOK_DEV = 384
SEQLEN = 49152
NBLK = 384
N_SEQ = 128


def draw_levels(key, part):
    order = jax.random.permutation(jax.random.fold_in(key, 7), NLEV - 1)
    chosen = order[:SAMPLES].astype(jnp.int32)
    top_slot = jax.random.randint(jax.random.fold_in(key, 9), (), 0, SAMPLES, dtype=jnp.int32)
    slots = jnp.arange(SAMPLES, dtype=jnp.int32)
    return jnp.where(slots == top_slot, jnp.int32(NLEV - 1), chosen).astype(jnp.int32)


def draw_pairs(key, part):
    blocks_dev = TOK_DEV // BLOCK
    block_ids = jnp.arange(NBLK, dtype=jnp.int32)
    owners = block_ids // blocks_dev
    columns = []
    for section_idx in range(SECTIONS):
        shifts = jax.random.randint(jax.random.fold_in(key, 11 + section_idx), (N_SEQ,), 0, blocks_dev, dtype=jnp.int32)
        partner = jnp.bitwise_xor(owners, N_SEQ // 2 ** (section_idx + 1))
        offsets = (block_ids % blocks_dev + shifts[owners]) % blocks_dev
        columns.append(partner * blocks_dev + offsets)
    return jnp.stack(columns, axis=1).astype(jnp.int32)


def draw_w_qkv(key, part):
    base = jax.random.truncated_normal(jax.random.fold_in(key, 3), -4.0, 4.0, (3, D, D), jnp.float32)
    factors = jnp.array([2.0, 2.0, 1.0], jnp.float32) / math.sqrt(D)
    return (base * factors[:, None, None]).astype(jnp.bfloat16)


def level_of(key, shape, split, low, high):
    factor_of, own = 1.0, jax.random.fold_in(key, 6)
    for dim, shards_of in split:
        steps = jnp.exp(jax.random.uniform(jax.random.fold_in(own, dim), (shards_of,), jnp.float32, low / len(split), high / len(split)))
        factor_of = factor_of * jnp.repeat(steps, shape[dim] // shards_of).reshape([-1 if axis == dim else 1 for axis in range(len(shape))])
    return factor_of


def centred(key, shape, deviation, reach, split=(), kind=jnp.bfloat16):
    entries = jax.random.normal(key, shape, jnp.float32) * deviation
    if len(split) > 0:
        entries = level_of(key, shape, split, -0.22, 0.18) * entries
    return jnp.clip(entries, min=-reach, max=reach).astype(kind)


def setup_inputs(seed: int = 0) -> dict:
    splits = jax.random.split(jax.random.key(seed), 8)
    return {
        "noisy": centred(splits[0], (SAMPLES, SEQLEN, D), 1.0, 6.0, ((1, 128), (2, 2))),
        "levels": draw_levels(jax.random.fold_in(splits[7], 71), 0),
        "pairs": draw_pairs(jax.random.fold_in(splits[7], 71), 0),
        "w_qkv": draw_w_qkv(jax.random.fold_in(splits[7], 71), 0),
        "w_out": centred(splits[4], (D, D), D ** -0.5, 0.1875, ((0, 2),)),
        "w_up": centred(splits[5], (D, FF), D ** -0.5, 0.1875, ((1, 2),)),
        "w_down": centred(splits[6], (FF, D), FF ** -0.5, 0.109375, ((0, 2),)),
    }


def level_features(levels, model_width):
    half_count = model_width // 2
    index_row = jnp.arange(half_count, dtype=jnp.float32)
    freqs = jnp.exp(-math.log(10000.0) * index_row / half_count)
    angles = levels.astype(jnp.float32)[:, None] * freqs[None, :]
    return jnp.concatenate([jnp.sin(angles), jnp.cos(angles)], axis=1)

def rms_norm(values):
    return values * lax.rsqrt(lax.optimization_barrier(jnp.mean(values * values, axis=-1, keepdims=True)) + 1e-06)

def reference(noisy, levels, pairs, w_qkv, w_out, w_up, w_down):
    samples, seqlen, model_width = noisy.shape
    level_feat = level_features(levels, model_width)
    normed = (rms_norm(noisy.astype(jnp.float32)) + level_feat[:, None, :]).astype(jnp.bfloat16)
    flat = normed.reshape(samples * seqlen, model_width)
    projected = [jnp.dot(flat, w_qkv[which], preferred_element_type=jnp.float32).astype(jnp.bfloat16).reshape(samples, seqlen, model_width) for which in range(3)]
    queries, key_rows, value_rows = projected
    nblocks = seqlen // BLOCK
    blocks_dev = TOK_DEV // BLOCK
    head_dim = model_width // HEADS
    scale = 1.0 / math.sqrt(head_dim)
    zero_idx = jnp.int32(0)

    def denoise_block(item_idx):
        sample_idx = (item_idx // nblocks).astype(jnp.int32)
        block_idx = (item_idx % nblocks).astype(jnp.int32)
        start = (block_idx * BLOCK).astype(jnp.int32)
        group_start = (block_idx // blocks_dev * TOK_DEV).astype(jnp.int32)
        query_block = lax.dynamic_slice(queries, (sample_idx, start, zero_idx), (1, BLOCK, model_width))[0]
        key_parts = [lax.dynamic_slice(key_rows, (sample_idx, group_start, zero_idx), (1, TOK_DEV, model_width))[0]]
        value_parts = [lax.dynamic_slice(value_rows, (sample_idx, group_start, zero_idx), (1, TOK_DEV, model_width))[0]]
        for section_idx in range(SECTIONS):
            far_start = (pairs[block_idx, section_idx] * BLOCK).astype(jnp.int32)
            key_parts.append(lax.dynamic_slice(key_rows, (sample_idx, far_start, zero_idx), (1, BLOCK, model_width))[0])
            value_parts.append(lax.dynamic_slice(value_rows, (sample_idx, far_start, zero_idx), (1, BLOCK, model_width))[0])
        key_set = jnp.concatenate(key_parts, axis=0).astype(jnp.float32).reshape(-1, HEADS, head_dim)
        value_set = jnp.concatenate(value_parts, axis=0).astype(jnp.float32).reshape(-1, HEADS, head_dim)
        query_heads = query_block.astype(jnp.float32).reshape(BLOCK, HEADS, head_dim)
        scores = jnp.einsum('qhd,khd->hqk', query_heads, key_set) * scale
        probs = jax.nn.softmax(scores, axis=-1).astype(jnp.bfloat16)
        mixed = jnp.einsum('hqk,khd->qhd', probs.astype(jnp.float32), value_set).astype(jnp.bfloat16).reshape(BLOCK, model_width)
        inputs = lax.dynamic_slice(noisy, (sample_idx, start, zero_idx), (1, BLOCK, model_width))[0].astype(jnp.float32)
        middle = (inputs + jnp.dot(mixed, w_out, preferred_element_type=jnp.float32)).astype(jnp.bfloat16)
        inner = rms_norm(middle.astype(jnp.float32)).astype(jnp.bfloat16)
        hidden = jax.nn.gelu(jnp.dot(inner, w_up, preferred_element_type=jnp.float32), approximate=True).astype(jnp.bfloat16)
        return (middle.astype(jnp.float32) + jnp.dot(hidden, w_down, preferred_element_type=jnp.float32)).astype(jnp.bfloat16)
    items = jnp.arange(samples * nblocks, dtype=jnp.int32)
    result = lax.map(denoise_block, items)
    return result.reshape(samples, seqlen, model_width)
```

```python
import math

import jax
import jax.numpy as jnp
from jax import lax
from jax.sharding import PartitionSpec as P


D = 1024
HEADS = 16
BLOCK = 128
SECTIONS = 4


def partner(x, axis, stride):
    return lax.ppermute(x, axis, [(i, i ^ 1 << stride) for i in range(lax.axis_size(axis))])


def tp_swap(x):
    return lax.ppermute(x, "tp", [(0, 1), (1, 0)])


def tp_join(own, other, tp_index):
    first = jnp.where(tp_index == 0, own, other)
    second = jnp.where(tp_index == 0, other, own)
    return jnp.concatenate([first, second], axis=-1)


def tp_half(x, index, width):
    return lax.dynamic_slice_in_dim(x, index * width, width, axis=x.ndim - 1)


def level_features(levels, model_width):
    half_count = model_width // 2
    index_row = jnp.arange(half_count, dtype=jnp.float32)
    freqs = jnp.exp(-math.log(10000.0) * index_row / half_count)
    angles = levels.astype(jnp.float32)[:, None] * freqs[None, :]
    return jnp.concatenate([jnp.sin(angles), jnp.cos(angles)], axis=1)


def rms_norm(values):
    return values * lax.rsqrt(jnp.mean(values * values, axis=-1, keepdims=True) + 1e-06)


def condition(gathered, level_feat):
    return (rms_norm(gathered.astype(jnp.float32)) + level_feat[:, None, :]).astype(jnp.bfloat16)


def per_device(noisy, levels, pairs, w_qkv, w_out, w_up, w_down):
    samples, tok_rows, half_width = noisy.shape
    tp_index = lax.axis_index("tp")
    noisy_other = tp_swap(noisy)
    gathered = tp_join(noisy, noisy_other, tp_index)
    model_width = gathered.shape[2]
    level_feat = level_features(levels, model_width)
    normed = condition(gathered, level_feat)
    projected = jnp.einsum(
        "std,cde->cste", normed, w_qkv, preferred_element_type=jnp.float32
    ).astype(jnp.bfloat16)
    queries, keys_here, values_here = (projected[0], projected[1], projected[2])
    blocks_dev = tok_rows // BLOCK
    head_dim = D // HEADS
    local_width = w_qkv.shape[2]
    local_heads = local_width // head_dim
    axis_bits = lax.axis_size("seq").bit_length() - 1
    kv_here = jnp.stack([keys_here, values_here])
    far_keys = []
    far_values = []
    for section_idx in range(SECTIONS):
        bit_pos = axis_bits - 1 - section_idx
        got_kv = partner(kv_here, "seq", bit_pos)
        got_keys, got_values = got_kv[0], got_kv[1]
        offset = pairs[:, section_idx] % blocks_dev
        far_keys.append(
            jnp.take(got_keys.reshape(samples, blocks_dev, BLOCK, local_width), offset, axis=1)
        )
        far_values.append(
            jnp.take(got_values.reshape(samples, blocks_dev, BLOCK, local_width), offset, axis=1)
        )
    far_count = SECTIONS * BLOCK
    key_far = jnp.concatenate(far_keys, axis=2).reshape(
        samples, blocks_dev, far_count, local_heads, head_dim
    )
    value_far = jnp.concatenate(far_values, axis=2).reshape(
        samples, blocks_dev, far_count, local_heads, head_dim
    )
    query_heads = queries.reshape(samples, blocks_dev, BLOCK, local_heads, head_dim)
    key_near = keys_here.reshape(samples, tok_rows, local_heads, head_dim)
    value_near = values_here.reshape(samples, tok_rows, local_heads, head_dim)
    scale = 1.0 / math.sqrt(head_dim)
    near_scores = jnp.einsum(
        "sbqhd,skhd->sbhqk", query_heads, key_near, preferred_element_type=jnp.float32
    )
    far_scores = jnp.einsum(
        "sbqhd,sbkhd->sbhqk", query_heads, key_far, preferred_element_type=jnp.float32
    )
    scores = jnp.concatenate([near_scores, far_scores], axis=-1) * scale
    probs = jax.nn.softmax(scores, axis=-1).astype(jnp.bfloat16)
    mixed = jnp.einsum(
        "sbhqk,skhd->sbqhd", probs[..., :tok_rows], value_near, preferred_element_type=jnp.float32
    )
    mixed = mixed + jnp.einsum(
        "sbhqk,sbkhd->sbqhd", probs[..., tok_rows:], value_far, preferred_element_type=jnp.float32
    )
    mixed = mixed.astype(jnp.bfloat16).reshape(samples, tok_rows, local_width)
    attn_part = jnp.einsum("sth,hd->std", mixed, w_out, preferred_element_type=jnp.float32)
    attn_own = attn_part.astype(jnp.bfloat16)
    attn_other = tp_swap(attn_own)
    attn_sum = attn_own.astype(jnp.float32) + attn_other.astype(jnp.float32)
    middle = (gathered.astype(jnp.float32) + attn_sum).astype(jnp.bfloat16)
    middle_half = tp_half(middle, tp_index, half_width)
    inner = rms_norm(middle.astype(jnp.float32)).astype(jnp.bfloat16)
    hidden = jax.nn.gelu(
        jnp.einsum("std,df->stf", inner, w_up, preferred_element_type=jnp.float32), approximate=True
    ).astype(jnp.bfloat16)
    down_part = jnp.einsum("stf,fd->std", hidden, w_down, preferred_element_type=jnp.float32)
    down_own = tp_half(down_part, tp_index, half_width)
    down_send = tp_half(down_part, 1 - tp_index, half_width).astype(jnp.bfloat16)
    down_half = down_own + tp_swap(down_send).astype(jnp.float32)
    return (middle_half.astype(jnp.float32) + down_half).astype(jnp.bfloat16)


def solution(mesh):
    in_specs = (
        P(None, "seq", "tp"),
        P(),
        P("seq", None),
        P(None, None, "tp"),
        P("tp", None),
        P(None, "tp"),
        P("tp", None),
    )
    out_specs = P(None, "seq", "tp")
    return jax.shard_map(
        per_device, mesh=mesh, in_specs=in_specs, out_specs=out_specs, check_vma=False
    )
```

```python
import functools
import math

import jax
import jax.numpy as jnp
from jax import lax
from jax.experimental import pallas as pl
from jax.experimental.pallas import tpu as pltpu
from jax.sharding import PartitionSpec as P


D = 1024
HEADS = 16
BLOCK = 128
SECTIONS = 4


def partner(x, axis, stride):
    return lax.ppermute(x, axis, [(i, i ^ 1 << stride) for i in range(lax.axis_size(axis))])


def tp_swap(x):
    return lax.ppermute(x, "tp", [(0, 1), (1, 0)])


def tp_join(own, other, tp_index):
    first = jnp.where(tp_index == 0, own, other)
    second = jnp.where(tp_index == 0, other, own)
    return jnp.concatenate([first, second], axis=-1)


def tp_half(x, index, width):
    return lax.dynamic_slice_in_dim(x, index * width, width, axis=x.ndim - 1)


def attention_kernel(off_ref, q_ref, kn_ref, vn_ref, *refs, heads, head_dim):
    far_k = refs[0:2 * SECTIONS:2]
    far_v = refs[1:2 * SECTIONS:2]
    out_ref = refs[2 * SECTIONS]
    scale = 1.0 / math.sqrt(head_dim)
    dims = (((1,), (1,)), ((), ()))
    for h in range(heads):
        cols = slice(h * head_dim, (h + 1) * head_dim)
        q = q_ref[0, :, cols]
        keys = [kn_ref[0, 0, :, cols]] + [r[0, 0, 0, :, cols] for r in far_k]
        vals = [vn_ref[0, 0, :, cols]] + [r[0, 0, 0, :, cols] for r in far_v]
        key_set = jnp.concatenate(keys, axis=0)
        val_set = jnp.concatenate(vals, axis=0)
        scores = lax.dot_general(q, key_set, dims, preferred_element_type=jnp.float32) * scale
        top = jnp.max(scores, axis=-1, keepdims=True)
        expd = jnp.exp(scores - top)
        probs = (expd / jnp.sum(expd, axis=-1, keepdims=True)).astype(jnp.bfloat16)
        mixed = jnp.dot(probs, val_set, preferred_element_type=jnp.float32)
        out_ref[0, :, cols] = mixed.astype(out_ref.dtype)


def block_attention(queries, kv_here, got, offsets, heads, head_dim):
    samples, tok_rows, width = queries.shape
    blocks_dev = tok_rows // BLOCK
    in_specs = [
        pl.BlockSpec((1, BLOCK, width), lambda s, b, off: (s, b, 0)),
        pl.BlockSpec((1, 1, tok_rows, width), lambda s, b, off: (0, s, 0, 0)),
        pl.BlockSpec((1, 1, tok_rows, width), lambda s, b, off: (1, s, 0, 0)),
    ]
    operands = [queries, kv_here, kv_here]
    for section_idx in range(SECTIONS):
        for which in range(2):
            in_specs.append(
                pl.BlockSpec(
                    (1, 1, 1, BLOCK, width),
                    lambda s, b, off, w=which, c=section_idx: (w, s, off[b * SECTIONS + c], 0, 0),
                )
            )
            operands.append(got[section_idx])
    grid_spec = pltpu.PrefetchScalarGridSpec(
        num_scalar_prefetch=1,
        grid=(samples, blocks_dev),
        in_specs=in_specs,
        out_specs=pl.BlockSpec((1, BLOCK, width), lambda s, b, off: (s, b, 0)),
    )
    return pl.pallas_call(
        functools.partial(attention_kernel, heads=heads, head_dim=head_dim),
        grid_spec=grid_spec,
        out_shape=jax.ShapeDtypeStruct(queries.shape, queries.dtype),
    )(offsets, *operands)


def level_features(levels, model_width):
    half_count = model_width // 2
    index_row = jnp.arange(half_count, dtype=jnp.float32)
    freqs = jnp.exp(-math.log(10000.0) * index_row / half_count)
    angles = levels.astype(jnp.float32)[:, None] * freqs[None, :]
    return jnp.concatenate([jnp.sin(angles), jnp.cos(angles)], axis=1)


def rms_norm(values):
    return values * lax.rsqrt(jnp.mean(values * values, axis=-1, keepdims=True) + 1e-06)


def condition(gathered, level_feat):
    return (rms_norm(gathered.astype(jnp.float32)) + level_feat[:, None, :]).astype(jnp.bfloat16)


def per_device(noisy, levels, pairs, w_qkv, w_out, w_up, w_down):
    samples, tok_rows, half_width = noisy.shape
    tp_index = lax.axis_index("tp")
    noisy_other = tp_swap(noisy)
    gathered = tp_join(noisy, noisy_other, tp_index)
    model_width = gathered.shape[2]
    level_feat = level_features(levels, model_width)
    normed = condition(gathered, level_feat)
    projected = jnp.einsum(
        "std,cde->cste", normed, w_qkv, preferred_element_type=jnp.float32
    ).astype(jnp.bfloat16)
    queries, keys_here, values_here = (projected[0], projected[1], projected[2])
    blocks_dev = tok_rows // BLOCK
    head_dim = D // HEADS
    local_width = w_qkv.shape[2]
    local_heads = local_width // head_dim
    axis_bits = lax.axis_size("seq").bit_length() - 1
    kv_here = jnp.stack([keys_here, values_here])
    offsets = (pairs % blocks_dev).astype(jnp.int32).reshape(-1)
    got = []
    for section_idx in range(SECTIONS):
        bit_pos = axis_bits - 1 - section_idx
        got.append(
            partner(kv_here, "seq", bit_pos).reshape(2, samples, blocks_dev, BLOCK, local_width)
        )
    mixed = block_attention(queries, kv_here, got, offsets, local_heads, head_dim)
    attn_part = jnp.einsum("sth,hd->std", mixed, w_out, preferred_element_type=jnp.float32)
    attn_own = attn_part.astype(jnp.bfloat16)
    attn_other = tp_swap(attn_own)
    attn_sum = attn_own.astype(jnp.float32) + attn_other.astype(jnp.float32)
    middle = (gathered.astype(jnp.float32) + attn_sum).astype(jnp.bfloat16)
    middle_half = tp_half(middle, tp_index, half_width)
    inner = rms_norm(middle.astype(jnp.float32)).astype(jnp.bfloat16)
    hidden = jax.nn.gelu(
        jnp.einsum("std,df->stf", inner, w_up, preferred_element_type=jnp.float32), approximate=True
    ).astype(jnp.bfloat16)
    down_part = jnp.einsum("stf,fd->std", hidden, w_down, preferred_element_type=jnp.float32)
    down_own = tp_half(down_part, tp_index, half_width)
    down_send = tp_half(down_part, 1 - tp_index, half_width).astype(jnp.bfloat16)
    down_half = down_own + tp_swap(down_send).astype(jnp.float32)
    return (middle_half.astype(jnp.float32) + down_half).astype(jnp.bfloat16)


def solution(mesh):
    in_specs = (
        P(None, "seq", "tp"),
        P(),
        P("seq", None),
        P(None, None, "tp"),
        P("tp", None),
        P(None, "tp"),
        P("tp", None),
    )
    out_specs = P(None, "seq", "tp")
    return jax.shard_map(
        per_device, mesh=mesh, in_specs=in_specs, out_specs=out_specs, check_vma=False
    )
```

```python
import functools
import math

import jax
import jax.numpy as jnp
from jax import lax
from jax.experimental import pallas as pl
from jax.experimental.pallas import tpu as pltpu
from jax.sharding import PartitionSpec as P


D = 1024
HEADS = 16
BLOCK = 128
SECTIONS = 4


def partner(x, axis, stride):
    return lax.ppermute(x, axis, [(i, i ^ 1 << stride) for i in range(lax.axis_size(axis))])


def tp_swap(x):
    return lax.ppermute(x, "tp", [(0, 1), (1, 0)])


def tp_join(own, other, tp_index):
    first = jnp.where(tp_index == 0, own, other)
    second = jnp.where(tp_index == 0, other, own)
    return jnp.concatenate([first, second], axis=-1)


def tp_half(x, index, width):
    return lax.dynamic_slice_in_dim(x, index * width, width, axis=x.ndim - 1)


def attention_kernel(off_ref, q_ref, kn_ref, vn_ref, *refs, heads, head_dim):
    far_k = refs[0:2 * SECTIONS:2]
    far_v = refs[1:2 * SECTIONS:2]
    out_ref = refs[2 * SECTIONS]
    scale = 1.0 / math.sqrt(head_dim)
    dims = (((1,), (1,)), ((), ()))
    for h in range(heads):
        cols = slice(h * head_dim, (h + 1) * head_dim)
        q = q_ref[0, :, cols]
        keys = [kn_ref[0, 0, :, cols]] + [r[0, 0, 0, :, cols] for r in far_k]
        vals = [vn_ref[0, 0, :, cols]] + [r[0, 0, 0, :, cols] for r in far_v]
        key_set = jnp.concatenate(keys, axis=0)
        val_set = jnp.concatenate(vals, axis=0)
        scores = lax.dot_general(q, key_set, dims, preferred_element_type=jnp.float32) * scale
        top = jnp.max(scores, axis=-1, keepdims=True)
        expd = jnp.exp(scores - top)
        probs = (expd / jnp.sum(expd, axis=-1, keepdims=True)).astype(jnp.bfloat16)
        mixed = jnp.dot(probs, val_set, preferred_element_type=jnp.float32)
        out_ref[0, :, cols] = mixed.astype(out_ref.dtype)


def block_attention(queries, kv_here, got, offsets, heads, head_dim):
    samples, tok_rows, width = queries.shape
    blocks_dev = tok_rows // BLOCK
    in_specs = [
        pl.BlockSpec((1, BLOCK, width), lambda s, b, off: (s, b, 0)),
        pl.BlockSpec((1, 1, tok_rows, width), lambda s, b, off: (0, s, 0, 0)),
        pl.BlockSpec((1, 1, tok_rows, width), lambda s, b, off: (1, s, 0, 0)),
    ]
    operands = [queries, kv_here, kv_here]
    for section_idx in range(SECTIONS):
        for which in range(2):
            in_specs.append(
                pl.BlockSpec(
                    (1, 1, 1, BLOCK, width),
                    lambda s, b, off, w=which, c=section_idx: (w, s, off[b * SECTIONS + c], 0, 0),
                )
            )
            operands.append(got[section_idx])
    grid_spec = pltpu.PrefetchScalarGridSpec(
        num_scalar_prefetch=1,
        grid=(samples, blocks_dev),
        in_specs=in_specs,
        out_specs=pl.BlockSpec((1, BLOCK, width), lambda s, b, off: (s, b, 0)),
    )
    return pl.pallas_call(
        functools.partial(attention_kernel, heads=heads, head_dim=head_dim),
        grid_spec=grid_spec,
        out_shape=jax.ShapeDtypeStruct(queries.shape, queries.dtype),
    )(offsets, *operands)


def level_features(levels, model_width):
    half_count = model_width // 2
    index_row = jnp.arange(half_count, dtype=jnp.float32)
    freqs = jnp.exp(-math.log(10000.0) * index_row / half_count)
    angles = levels.astype(jnp.float32)[:, None] * freqs[None, :]
    return jnp.concatenate([jnp.sin(angles), jnp.cos(angles)], axis=1)


def rms_norm(values):
    return values * lax.rsqrt(jnp.mean(values * values, axis=-1, keepdims=True) + 1e-06)


def condition(gathered, level_feat):
    return (rms_norm(gathered.astype(jnp.float32)) + level_feat[:, None, :]).astype(jnp.bfloat16)


def per_device(noisy, levels, pairs, w_qkv, w_out, w_up, w_down):
    level_feat = level_features(levels, D)
    outs = [
        one_sample(noisy[s:s + 1], level_feat[s:s + 1], pairs, w_qkv, w_out, w_up, w_down)
        for s in range(noisy.shape[0])
    ]
    return jnp.concatenate(outs, axis=0)


def one_sample(noisy, level_feat, pairs, w_qkv, w_out, w_up, w_down):
    samples, tok_rows, half_width = noisy.shape
    tp_index = lax.axis_index("tp")
    noisy_other = tp_swap(noisy)
    gathered = tp_join(noisy, noisy_other, tp_index)
    normed = condition(gathered, level_feat)
    projected = jnp.einsum(
        "std,cde->cste", normed, w_qkv, preferred_element_type=jnp.float32
    ).astype(jnp.bfloat16)
    queries, keys_here, values_here = (projected[0], projected[1], projected[2])
    blocks_dev = tok_rows // BLOCK
    head_dim = D // HEADS
    local_width = w_qkv.shape[2]
    local_heads = local_width // head_dim
    axis_bits = lax.axis_size("seq").bit_length() - 1
    kv_here = jnp.stack([keys_here, values_here])
    offsets = (pairs % blocks_dev).astype(jnp.int32).reshape(-1)
    got = []
    for section_idx in range(SECTIONS):
        bit_pos = axis_bits - 1 - section_idx
        got.append(
            partner(kv_here, "seq", bit_pos).reshape(2, samples, blocks_dev, BLOCK, local_width)
        )
    mixed = block_attention(queries, kv_here, got, offsets, local_heads, head_dim)
    attn_part = jnp.einsum("sth,hd->std", mixed, w_out, preferred_element_type=jnp.float32)
    attn_own = attn_part.astype(jnp.bfloat16)
    attn_other = tp_swap(attn_own)
    attn_sum = attn_own.astype(jnp.float32) + attn_other.astype(jnp.float32)
    middle = (gathered.astype(jnp.float32) + attn_sum).astype(jnp.bfloat16)
    middle_half = tp_half(middle, tp_index, half_width)
    inner = rms_norm(middle.astype(jnp.float32)).astype(jnp.bfloat16)
    hidden = jax.nn.gelu(
        jnp.einsum("std,df->stf", inner, w_up, preferred_element_type=jnp.float32), approximate=True
    ).astype(jnp.bfloat16)
    down_part = jnp.einsum("stf,fd->std", hidden, w_down, preferred_element_type=jnp.float32)
    down_own = tp_half(down_part, tp_index, half_width)
    down_send = tp_half(down_part, 1 - tp_index, half_width).astype(jnp.bfloat16)
    down_half = down_own + tp_swap(down_send).astype(jnp.float32)
    return (middle_half.astype(jnp.float32) + down_half).astype(jnp.bfloat16)


def solution(mesh):
    in_specs = (
        P(None, "seq", "tp"),
        P(),
        P("seq", None),
        P(None, None, "tp"),
        P("tp", None),
        P(None, "tp"),
        P("tp", None),
    )
    out_specs = P(None, "seq", "tp")
    return jax.shard_map(
        per_device, mesh=mesh, in_specs=in_specs, out_specs=out_specs, check_vma=False
    )
```

```python
import functools
import math

import jax
import jax.numpy as jnp
from jax import lax
from jax.experimental import pallas as pl
from jax.experimental.pallas import tpu as pltpu
from jax.sharding import PartitionSpec as P


D = 1024
HEADS = 16
BLOCK = 128
SECTIONS = 4


def partner(x, axis, stride):
    return lax.ppermute(x, axis, [(i, i ^ 1 << stride) for i in range(lax.axis_size(axis))])


def tp_swap(x):
    return lax.ppermute(x, "tp", [(0, 1), (1, 0)])


def tp_join(own, other, tp_index):
    first = jnp.where(tp_index == 0, own, other)
    second = jnp.where(tp_index == 0, other, own)
    return jnp.concatenate([first, second], axis=-1)


def tp_half(x, index, width):
    return lax.dynamic_slice_in_dim(x, index * width, width, axis=x.ndim - 1)


def attention_kernel(off_ref, q_ref, kn_ref, vn_ref, *refs, head_dim):
    far_k = refs[0:2 * SECTIONS:2]
    far_v = refs[1:2 * SECTIONS:2]
    out_ref = refs[2 * SECTIONS]
    scale = 1.0 / math.sqrt(head_dim)
    dims = (((1,), (1,)), ((), ()))
    q = q_ref[0]
    tok_rows = q.shape[0]
    key_near = kn_ref[0, 0]
    value_near = vn_ref[0, 0]
    first = lax.broadcasted_iota(jnp.int32, q.shape, 1) < head_dim
    far_keys = []
    far_values = []
    for b in range(tok_rows // BLOCK):
        picks = [off_ref[b * SECTIONS + c] for c in range(SECTIONS)]
        far_keys.append(jnp.concatenate([far_k[c][0, 0, picks[c]] for c in range(SECTIONS)], axis=0))
        far_values.append(jnp.concatenate([far_v[c][0, 0, picks[c]] for c in range(SECTIONS)], axis=0))
    halves = []
    for own in (first, jnp.logical_not(first)):
        q_head = jnp.where(own, q, jnp.zeros_like(q))
        near_scores = lax.dot_general(q_head, key_near, dims, preferred_element_type=jnp.float32) * scale
        near_probs = []
        far_mixed = []
        for b in range(tok_rows // BLOCK):
            rows = slice(b * BLOCK, (b + 1) * BLOCK)
            near_b = near_scores[rows]
            far_b = lax.dot_general(
                q_head[rows], far_keys[b], dims, preferred_element_type=jnp.float32
            ) * scale
            top = jnp.maximum(near_b.max(axis=-1, keepdims=True), far_b.max(axis=-1, keepdims=True))
            near_e = jnp.exp(near_b - top)
            far_e = jnp.exp(far_b - top)
            total = near_e.sum(axis=-1, keepdims=True) + far_e.sum(axis=-1, keepdims=True)
            near_probs.append((near_e / total).astype(jnp.bfloat16))
            far_mixed.append(
                jnp.dot((far_e / total).astype(jnp.bfloat16), far_values[b],
                        preferred_element_type=jnp.float32)
            )
        mixed = jnp.dot(
            jnp.concatenate(near_probs, axis=0), value_near, preferred_element_type=jnp.float32
        ) + jnp.concatenate(far_mixed, axis=0)
        halves.append(mixed)
    out_ref[0] = jnp.where(first, halves[0], halves[1]).astype(out_ref.dtype)


def block_attention(queries, kv_here, got, offsets, head_dim):
    _, tok_rows, width = queries.shape
    blocks_dev = tok_rows // BLOCK
    lanes = 2 * head_dim
    in_specs = [
        pl.BlockSpec((1, tok_rows, lanes), lambda j, off: (0, 0, j)),
        pl.BlockSpec((1, 1, tok_rows, lanes), lambda j, off: (0, 0, 0, j)),
        pl.BlockSpec((1, 1, tok_rows, lanes), lambda j, off: (1, 0, 0, j)),
    ]
    operands = [queries, kv_here, kv_here]
    for section_idx in range(SECTIONS):
        for which in range(2):
            in_specs.append(
                pl.BlockSpec(
                    (1, 1, blocks_dev, BLOCK, lanes),
                    lambda j, off, w=which: (w, 0, 0, 0, j),
                )
            )
            operands.append(got[section_idx])
    grid_spec = pltpu.PrefetchScalarGridSpec(
        num_scalar_prefetch=1,
        grid=(width // lanes,),
        in_specs=in_specs,
        out_specs=pl.BlockSpec((1, tok_rows, lanes), lambda j, off: (0, 0, j)),
    )
    return pl.pallas_call(
        functools.partial(attention_kernel, head_dim=head_dim),
        grid_spec=grid_spec,
        out_shape=jax.ShapeDtypeStruct(queries.shape, queries.dtype),
    )(offsets, *operands)


def level_features(levels, model_width):
    half_count = model_width // 2
    index_row = jnp.arange(half_count, dtype=jnp.float32)
    freqs = jnp.exp(-math.log(10000.0) * index_row / half_count)
    angles = levels.astype(jnp.float32)[:, None] * freqs[None, :]
    return jnp.concatenate([jnp.sin(angles), jnp.cos(angles)], axis=1)


def rms_norm(values):
    return values * lax.rsqrt(jnp.mean(values * values, axis=-1, keepdims=True) + 1e-06)


def condition(gathered, level_feat):
    return (rms_norm(gathered.astype(jnp.float32)) + level_feat[:, None, :]).astype(jnp.bfloat16)


def per_device(noisy, levels, pairs, w_qkv, w_out, w_up, w_down):
    level_feat = level_features(levels, D)
    outs = []
    for s in range(noisy.shape[0]):
        outs.append(
            one_sample(noisy[s:s + 1], level_feat[s:s + 1], pairs, w_qkv, w_out, w_up, w_down)
        )
    return jnp.concatenate(outs, axis=0)


def one_sample(noisy, level_feat, pairs, w_qkv, w_out, w_up, w_down):
    samples, tok_rows, half_width = noisy.shape
    tp_index = lax.axis_index("tp")
    noisy_other = tp_swap(noisy)
    gathered = tp_join(noisy, noisy_other, tp_index)
    normed = condition(gathered, level_feat)
    projected = jnp.einsum(
        "std,cde->cste", normed, w_qkv, preferred_element_type=jnp.float32
    ).astype(jnp.bfloat16)
    queries, keys_here, values_here = (projected[0], projected[1], projected[2])
    blocks_dev = tok_rows // BLOCK
    head_dim = D // HEADS
    local_width = w_qkv.shape[2]
    axis_bits = lax.axis_size("seq").bit_length() - 1
    kv_here = jnp.stack([keys_here, values_here])
    offsets = (pairs % blocks_dev).astype(jnp.int32).reshape(-1)
    got = []
    for section_idx in range(SECTIONS):
        bit_pos = axis_bits - 1 - section_idx
        got.append(
            partner(kv_here, "seq", bit_pos).reshape(2, samples, blocks_dev, BLOCK, local_width)
        )
    mixed = block_attention(queries, kv_here, got, offsets, head_dim)
    outs = []
    for chunk in range(blocks_dev):
        rows = slice(chunk * BLOCK, (chunk + 1) * BLOCK)
        outs.append(
            finish_rows(mixed[:, rows], gathered[:, rows], tp_index, half_width, w_out, w_up, w_down)
        )
    return jnp.concatenate(outs, axis=1)


def finish_rows(mixed, gathered, tp_index, half_width, w_out, w_up, w_down):
    attn_part = jnp.einsum("sth,hd->std", mixed, w_out, preferred_element_type=jnp.float32)
    attn_own = attn_part.astype(jnp.bfloat16)
    attn_other = tp_swap(attn_own)
    attn_sum = attn_own.astype(jnp.float32) + attn_other.astype(jnp.float32)
    middle = (gathered.astype(jnp.float32) + attn_sum).astype(jnp.bfloat16)
    middle_half = tp_half(middle, tp_index, half_width)
    inner = rms_norm(middle.astype(jnp.float32)).astype(jnp.bfloat16)
    hidden = jax.nn.gelu(
        jnp.einsum("std,df->stf", inner, w_up, preferred_element_type=jnp.float32), approximate=True
    ).astype(jnp.bfloat16)
    down_part = jnp.einsum("stf,fd->std", hidden, w_down, preferred_element_type=jnp.float32)
    down_own = tp_half(down_part, tp_index, half_width)
    down_send = tp_half(down_part, 1 - tp_index, half_width).astype(jnp.bfloat16)
    down_half = down_own + tp_swap(down_send).astype(jnp.float32)
    return (middle_half.astype(jnp.float32) + down_half).astype(jnp.bfloat16)


def solution(mesh):
    in_specs = (
        P(None, "seq", "tp"),
        P(),
        P("seq", None),
        P(None, None, "tp"),
        P("tp", None),
        P(None, "tp"),
        P("tp", None),
    )
    out_specs = P(None, "seq", "tp")
    return jax.shard_map(
        per_device, mesh=mesh, in_specs=in_specs, out_specs=out_specs, check_vma=False
    )
```

```python
import functools
import math

import jax
import jax.numpy as jnp
from jax import lax
from jax.experimental import pallas as pl
from jax.experimental.pallas import tpu as pltpu
from jax.sharding import PartitionSpec as P


D = 1024
HEADS = 16
BLOCK = 128
SECTIONS = 4


def partner(x, axis, stride):
    return lax.ppermute(x, axis, [(i, i ^ 1 << stride) for i in range(lax.axis_size(axis))])


def tp_swap(x):
    return lax.ppermute(x, "tp", [(0, 1), (1, 0)])


def tp_join(own, other, tp_index):
    first = jnp.where(tp_index == 0, own, other)
    second = jnp.where(tp_index == 0, other, own)
    return jnp.concatenate([first, second], axis=-1)


def tp_half(x, index, width):
    return lax.dynamic_slice_in_dim(x, index * width, width, axis=x.ndim - 1)


def attention_kernel(off_ref, q_ref, kn_ref, vn_ref, *refs, head_dim):
    far_k = refs[0:2 * SECTIONS:2]
    far_v = refs[1:2 * SECTIONS:2]
    out_ref = refs[2 * SECTIONS]
    scale = 1.0 / math.sqrt(head_dim)
    dims = (((1,), (1,)), ((), ()))
    q = q_ref[0]
    tok_rows = q.shape[0]
    key_near = kn_ref[0, 0]
    value_near = vn_ref[0, 0]
    first = lax.broadcasted_iota(jnp.int32, q.shape, 1) < head_dim
    far_keys = []
    far_values = []
    for b in range(tok_rows // BLOCK):
        picks = [off_ref[b * SECTIONS + c] for c in range(SECTIONS)]
        far_keys.append(jnp.concatenate([far_k[c][0, 0, picks[c]] for c in range(SECTIONS)], axis=0))
        far_values.append(jnp.concatenate([far_v[c][0, 0, picks[c]] for c in range(SECTIONS)], axis=0))
    halves = []
    for own in (first, jnp.logical_not(first)):
        q_head = jnp.where(own, q, jnp.zeros_like(q))
        near_scores = lax.dot_general(q_head, key_near, dims, preferred_element_type=jnp.float32) * scale
        near_probs = []
        far_mixed = []
        for b in range(tok_rows // BLOCK):
            rows = slice(b * BLOCK, (b + 1) * BLOCK)
            near_b = near_scores[rows]
            far_b = lax.dot_general(
                q_head[rows], far_keys[b], dims, preferred_element_type=jnp.float32
            ) * scale
            top = jnp.maximum(near_b.max(axis=-1, keepdims=True), far_b.max(axis=-1, keepdims=True))
            near_e = jnp.exp(near_b - top)
            far_e = jnp.exp(far_b - top)
            total = near_e.sum(axis=-1, keepdims=True) + far_e.sum(axis=-1, keepdims=True)
            near_probs.append((near_e / total).astype(jnp.bfloat16))
            far_mixed.append(
                jnp.dot((far_e / total).astype(jnp.bfloat16), far_values[b],
                        preferred_element_type=jnp.float32)
            )
        mixed = jnp.dot(
            jnp.concatenate(near_probs, axis=0), value_near, preferred_element_type=jnp.float32
        ) + jnp.concatenate(far_mixed, axis=0)
        halves.append(mixed)
    out_ref[0] = jnp.where(first, halves[0], halves[1]).astype(out_ref.dtype)


def block_attention(queries, kv_here, got, offsets, head_dim):
    _, tok_rows, width = queries.shape
    blocks_dev = tok_rows // BLOCK
    lanes = 2 * head_dim
    in_specs = [
        pl.BlockSpec((1, tok_rows, lanes), lambda j, off: (0, 0, j)),
        pl.BlockSpec((1, 1, tok_rows, lanes), lambda j, off: (0, 0, 0, j)),
        pl.BlockSpec((1, 1, tok_rows, lanes), lambda j, off: (1, 0, 0, j)),
    ]
    operands = [queries, kv_here, kv_here]
    for section_idx in range(SECTIONS):
        for which in range(2):
            in_specs.append(
                pl.BlockSpec(
                    (1, 1, blocks_dev, BLOCK, lanes),
                    lambda j, off, w=which: (w, 0, 0, 0, j),
                )
            )
            operands.append(got[section_idx])
    grid_spec = pltpu.PrefetchScalarGridSpec(
        num_scalar_prefetch=1,
        grid=(width // lanes,),
        in_specs=in_specs,
        out_specs=pl.BlockSpec((1, tok_rows, lanes), lambda j, off: (0, 0, j)),
    )
    return pl.pallas_call(
        functools.partial(attention_kernel, head_dim=head_dim),
        grid_spec=grid_spec,
        out_shape=jax.ShapeDtypeStruct(queries.shape, queries.dtype),
    )(offsets, *operands)


def level_features(levels, model_width):
    half_count = model_width // 2
    index_row = jnp.arange(half_count, dtype=jnp.float32)
    freqs = jnp.exp(-math.log(10000.0) * index_row / half_count)
    angles = levels.astype(jnp.float32)[:, None] * freqs[None, :]
    return jnp.concatenate([jnp.sin(angles), jnp.cos(angles)], axis=1)


def rms_norm(values):
    return values * lax.rsqrt(jnp.mean(values * values, axis=-1, keepdims=True) + 1e-06)


def condition(gathered, level_feat):
    return (rms_norm(gathered.astype(jnp.float32)) + level_feat[:, None, :]).astype(jnp.bfloat16)


def per_device(noisy, levels, pairs, w_qkv, w_out, w_up, w_down):
    level_feat = level_features(levels, D)
    outs = []
    for s in range(noisy.shape[0]):
        outs.append(
            one_sample(noisy[s:s + 1], level_feat[s:s + 1], pairs, w_qkv, w_out, w_up, w_down)
        )
    return jnp.concatenate(outs, axis=0)


def one_sample(noisy, level_feat, pairs, w_qkv, w_out, w_up, w_down):
    samples, tok_rows, half_width = noisy.shape
    tp_index = lax.axis_index("tp")
    noisy_other = tp_swap(noisy)
    gathered = tp_join(noisy, noisy_other, tp_index)
    normed = condition(gathered, level_feat)
    projected = jnp.einsum(
        "std,cde->cste", normed, w_qkv, preferred_element_type=jnp.float32
    ).astype(jnp.bfloat16)
    queries, keys_here, values_here = (projected[0], projected[1], projected[2])
    blocks_dev = tok_rows // BLOCK
    head_dim = D // HEADS
    local_width = w_qkv.shape[2]
    axis_bits = lax.axis_size("seq").bit_length() - 1
    kv_here = jnp.stack([keys_here, values_here])
    offsets = (pairs % blocks_dev).astype(jnp.int32).reshape(-1)
    got = []
    for section_idx in range(SECTIONS):
        bit_pos = axis_bits - 1 - section_idx
        got.append(
            partner(kv_here, "seq", bit_pos).reshape(2, samples, blocks_dev, BLOCK, local_width)
        )
    mixed = block_attention(queries, kv_here, got, offsets, head_dim)
    attn_part = jnp.einsum("sth,hd->std", mixed, w_out, preferred_element_type=jnp.float32)
    attn_own = attn_part.astype(jnp.bfloat16)
    attn_other = tp_swap(attn_own)
    attn_sum = attn_own.astype(jnp.float32) + attn_other.astype(jnp.float32)
    middle = (gathered.astype(jnp.float32) + attn_sum).astype(jnp.bfloat16)
    middle_half = tp_half(middle, tp_index, half_width)
    inner = rms_norm(middle.astype(jnp.float32)).astype(jnp.bfloat16)
    hidden = jax.nn.gelu(
        jnp.einsum("std,df->stf", inner, w_up, preferred_element_type=jnp.float32),
        approximate=True,
    ).astype(jnp.bfloat16)
    down_part = jnp.einsum("stf,fd->std", hidden, w_down, preferred_element_type=jnp.float32)
    down_own = tp_half(down_part, tp_index, half_width)
    down_send = tp_half(down_part, 1 - tp_index, half_width).astype(jnp.bfloat16)
    down_half = down_own + tp_swap(down_send).astype(jnp.float32)
    return (middle_half.astype(jnp.float32) + down_half).astype(jnp.bfloat16)


def solution(mesh):
    in_specs = (
        P(None, "seq", "tp"),
        P(),
        P("seq", None),
        P(None, None, "tp"),
        P("tp", None),
        P(None, "tp"),
        P("tp", None),
    )
    out_specs = P(None, "seq", "tp")
    return jax.shard_map(
        per_device, mesh=mesh, in_specs=in_specs, out_specs=out_specs, check_vma=False
    )
```

```python
import functools
import math

import jax
import jax.numpy as jnp
from jax import lax
from jax.experimental import pallas as pl
from jax.experimental.pallas import tpu as pltpu
from jax.sharding import PartitionSpec as P


D = 1024
HEADS = 16
BLOCK = 128
SECTIONS = 4


def partner(x, axis, stride):
    return lax.ppermute(x, axis, [(i, i ^ 1 << stride) for i in range(lax.axis_size(axis))])


def tp_swap(x):
    return lax.ppermute(x, "tp", [(0, 1), (1, 0)])


def full_w_out(w_out):
    seq_size = lax.axis_size("seq")
    tp_size = lax.axis_size("tp")
    far = seq_size // 2
    perm = [
        (s * tp_size + t, (s ^ far) * tp_size + (tp_size - 1 - t))
        for s in range(seq_size)
        for t in range(tp_size)
    ]
    other = lax.ppermute(w_out, ("seq", "tp"), perm)
    return tp_join(w_out, other, lax.axis_index("tp"), axis=0)


def tp_join(own, other, tp_index, axis=-1):
    first = jnp.where(tp_index == 0, own, other)
    second = jnp.where(tp_index == 0, other, own)
    return jnp.concatenate([first, second], axis=axis)


def tp_half(x, index, width):
    return lax.dynamic_slice_in_dim(x, index * width, width, axis=x.ndim - 1)


def attention_kernel(off_ref, q_ref, kn_ref, vn_ref, *refs, heads, head_dim):
    far_k = refs[0:2 * SECTIONS:2]
    far_v = refs[1:2 * SECTIONS:2]
    out_ref = refs[2 * SECTIONS]
    scale = 1.0 / math.sqrt(head_dim)
    dims = (((1,), (1,)), ((), ()))
    for h in range(heads):
        cols = slice(h * head_dim, (h + 1) * head_dim)
        q = q_ref[0, :, cols]
        keys = [kn_ref[0, 0, :, cols]] + [r[0, 0, 0, :, cols] for r in far_k]
        vals = [vn_ref[0, 0, :, cols]] + [r[0, 0, 0, :, cols] for r in far_v]
        key_set = jnp.concatenate(keys, axis=0)
        val_set = jnp.concatenate(vals, axis=0)
        scores = lax.dot_general(q, key_set, dims, preferred_element_type=jnp.float32) * scale
        top = jnp.max(scores, axis=-1, keepdims=True)
        expd = jnp.exp(scores - top)
        probs = (expd / jnp.sum(expd, axis=-1, keepdims=True)).astype(jnp.bfloat16)
        mixed = jnp.dot(probs, val_set, preferred_element_type=jnp.float32)
        out_ref[0, :, cols] = mixed.astype(out_ref.dtype)


def block_attention(queries, kv_here, got, offsets, heads, head_dim):
    samples, tok_rows, width = queries.shape
    blocks_dev = tok_rows // BLOCK
    in_specs = [
        pl.BlockSpec((1, BLOCK, width), lambda s, b, off: (s, b, 0)),
        pl.BlockSpec((1, 1, tok_rows, width), lambda s, b, off: (0, s, 0, 0)),
        pl.BlockSpec((1, 1, tok_rows, width), lambda s, b, off: (1, s, 0, 0)),
    ]
    operands = [queries, kv_here, kv_here]
    for section_idx in range(SECTIONS):
        for which in range(2):
            in_specs.append(
                pl.BlockSpec(
                    (1, 1, 1, BLOCK, width),
                    lambda s, b, off, w=which, c=section_idx: (w, s, off[b * SECTIONS + c], 0, 0),
                )
            )
            operands.append(got[section_idx])
    grid_spec = pltpu.PrefetchScalarGridSpec(
        num_scalar_prefetch=1,
        grid=(samples, blocks_dev),
        in_specs=in_specs,
        out_specs=pl.BlockSpec((1, BLOCK, width), lambda s, b, off: (s, b, 0)),
    )
    return pl.pallas_call(
        functools.partial(attention_kernel, heads=heads, head_dim=head_dim),
        grid_spec=grid_spec,
        out_shape=jax.ShapeDtypeStruct(queries.shape, queries.dtype),
    )(offsets, *operands)


def level_features(levels, model_width):
    half_count = model_width // 2
    index_row = jnp.arange(half_count, dtype=jnp.float32)
    freqs = jnp.exp(-math.log(10000.0) * index_row / half_count)
    angles = levels.astype(jnp.float32)[:, None] * freqs[None, :]
    return jnp.concatenate([jnp.sin(angles), jnp.cos(angles)], axis=1)


def rms_norm(values):
    return values * lax.rsqrt(jnp.mean(values * values, axis=-1, keepdims=True) + 1e-06)


def condition(gathered, level_feat):
    return (rms_norm(gathered.astype(jnp.float32)) + level_feat[:, None, :]).astype(jnp.bfloat16)


def per_device(noisy, levels, pairs, w_qkv, w_out, w_up, w_down):
    level_feat = level_features(levels, D)
    w_out = full_w_out(w_out)
    outs = [
        one_sample(noisy[s:s + 1], level_feat[s:s + 1], pairs, w_qkv, w_out, w_up, w_down)
        for s in range(noisy.shape[0])
    ]
    return jnp.concatenate(outs, axis=0)


def one_sample(noisy, level_feat, pairs, w_qkv, w_out, w_up, w_down):
    samples, tok_rows, half_width = noisy.shape
    tp_index = lax.axis_index("tp")
    noisy_other = tp_swap(noisy)
    gathered = tp_join(noisy, noisy_other, tp_index)
    normed = condition(gathered, level_feat)
    projected = jnp.einsum(
        "std,cde->cste", normed, w_qkv, preferred_element_type=jnp.float32
    ).astype(jnp.bfloat16)
    queries, keys_here, values_here = (projected[0], projected[1], projected[2])
    blocks_dev = tok_rows // BLOCK
    head_dim = D // HEADS
    local_width = w_qkv.shape[2]
    local_heads = local_width // head_dim
    axis_bits = lax.axis_size("seq").bit_length() - 1
    kv_here = jnp.stack([keys_here, values_here])
    offsets = (pairs % blocks_dev).astype(jnp.int32).reshape(-1)
    got = []
    for section_idx in range(SECTIONS):
        bit_pos = axis_bits - 1 - section_idx
        got.append(
            partner(kv_here, "seq", bit_pos).reshape(2, samples, blocks_dev, BLOCK, local_width)
        )
    mixed = block_attention(queries, kv_here, got, offsets, local_heads, head_dim)
    mixed_full = tp_join(mixed, tp_swap(mixed), tp_index)
    attn = jnp.einsum("sth,hd->std", mixed_full, w_out, preferred_element_type=jnp.float32)
    middle = (gathered.astype(jnp.float32) + attn).astype(jnp.bfloat16)
    middle_half = tp_half(middle, tp_index, half_width)
    inner = rms_norm(middle.astype(jnp.float32)).astype(jnp.bfloat16)
    hidden = jax.nn.gelu(
        jnp.einsum("std,df->stf", inner, w_up, preferred_element_type=jnp.float32), approximate=True
    ).astype(jnp.bfloat16)
    down_part = jnp.einsum("stf,fd->std", hidden, w_down, preferred_element_type=jnp.float32)
    down_own = tp_half(down_part, tp_index, half_width)
    down_send = tp_half(down_part, 1 - tp_index, half_width).astype(jnp.bfloat16)
    down_half = down_own + tp_swap(down_send).astype(jnp.float32)
    return (middle_half.astype(jnp.float32) + down_half).astype(jnp.bfloat16)


def solution(mesh):
    in_specs = (
        P(None, "seq", "tp"),
        P(),
        P("seq", None),
        P(None, None, "tp"),
        P("tp", None),
        P(None, "tp"),
        P("tp", None),
    )
    out_specs = P(None, "seq", "tp")
    return jax.shard_map(
        per_device, mesh=mesh, in_specs=in_specs, out_specs=out_specs, check_vma=False
    )
```

```python
import functools
import math

import jax
import jax.numpy as jnp
from jax import lax
from jax.experimental import pallas as pl
from jax.experimental.pallas import tpu as pltpu
from jax.sharding import PartitionSpec as P


D = 1024
HEADS = 16
BLOCK = 128
SECTIONS = 4


def partner(x, axis, stride):
    return lax.ppermute(x, axis, [(i, i ^ 1 << stride) for i in range(lax.axis_size(axis))])


def tp_swap(x):
    return lax.ppermute(x, "tp", [(0, 1), (1, 0)])


def other_w_out(w_out):
    seq_size = lax.axis_size("seq")
    tp_size = lax.axis_size("tp")
    far = seq_size // 2
    perm = [
        (s * tp_size + t, (s ^ far) * tp_size + (tp_size - 1 - t))
        for s in range(seq_size)
        for t in range(tp_size)
    ]
    return lax.ppermute(w_out, ("seq", "tp"), perm)


def tp_join(own, other, tp_index):
    first = jnp.where(tp_index == 0, own, other)
    second = jnp.where(tp_index == 0, other, own)
    return jnp.concatenate([first, second], axis=-1)


def tp_half(x, index, width):
    return lax.dynamic_slice_in_dim(x, index * width, width, axis=x.ndim - 1)


def attention_kernel(off_ref, q_ref, kn_ref, vn_ref, *refs, head_dim):
    far_k = refs[0:2 * SECTIONS:2]
    far_v = refs[1:2 * SECTIONS:2]
    out_ref = refs[2 * SECTIONS]
    scale = 1.0 / math.sqrt(head_dim)
    dims = (((1,), (1,)), ((), ()))
    q = q_ref[0]
    tok_rows = q.shape[0]
    key_near = kn_ref[0, 0]
    value_near = vn_ref[0, 0]
    first = lax.broadcasted_iota(jnp.int32, q.shape, 1) < head_dim
    far_keys = []
    far_values = []
    for b in range(tok_rows // BLOCK):
        picks = [off_ref[b * SECTIONS + c] for c in range(SECTIONS)]
        far_keys.append(jnp.concatenate([far_k[c][0, 0, picks[c]] for c in range(SECTIONS)], axis=0))
        far_values.append(jnp.concatenate([far_v[c][0, 0, picks[c]] for c in range(SECTIONS)], axis=0))
    halves = []
    for own in (first, jnp.logical_not(first)):
        q_head = jnp.where(own, q, jnp.zeros_like(q))
        near_scores = lax.dot_general(q_head, key_near, dims, preferred_element_type=jnp.float32) * scale
        near_probs = []
        far_mixed = []
        for b in range(tok_rows // BLOCK):
            rows = slice(b * BLOCK, (b + 1) * BLOCK)
            near_b = near_scores[rows]
            far_b = lax.dot_general(
                q_head[rows], far_keys[b], dims, preferred_element_type=jnp.float32
            ) * scale
            top = jnp.maximum(near_b.max(axis=-1, keepdims=True), far_b.max(axis=-1, keepdims=True))
            near_e = jnp.exp(near_b - top)
            far_e = jnp.exp(far_b - top)
            total = near_e.sum(axis=-1, keepdims=True) + far_e.sum(axis=-1, keepdims=True)
            near_probs.append((near_e / total).astype(jnp.bfloat16))
            far_mixed.append(
                jnp.dot((far_e / total).astype(jnp.bfloat16), far_values[b],
                        preferred_element_type=jnp.float32)
            )
        mixed = jnp.dot(
            jnp.concatenate(near_probs, axis=0), value_near, preferred_element_type=jnp.float32
        ) + jnp.concatenate(far_mixed, axis=0)
        halves.append(mixed)
    out_ref[0] = jnp.where(first, halves[0], halves[1]).astype(out_ref.dtype)


def block_attention(queries, kv_here, got, offsets, heads, head_dim):
    samples, tok_rows, width = queries.shape
    blocks_dev = tok_rows // BLOCK
    lanes = 2 * head_dim
    in_specs = [
        pl.BlockSpec((1, tok_rows, lanes), lambda j, off: (0, 0, j)),
        pl.BlockSpec((1, 1, tok_rows, lanes), lambda j, off: (0, 0, 0, j)),
        pl.BlockSpec((1, 1, tok_rows, lanes), lambda j, off: (1, 0, 0, j)),
    ]
    operands = [queries, kv_here, kv_here]
    for section_idx in range(SECTIONS):
        for which in range(2):
            in_specs.append(
                pl.BlockSpec(
                    (1, 1, blocks_dev, BLOCK, lanes),
                    lambda j, off, w=which: (w, 0, 0, 0, j),
                )
            )
            operands.append(got[section_idx])
    grid_spec = pltpu.PrefetchScalarGridSpec(
        num_scalar_prefetch=1,
        grid=(width // lanes,),
        in_specs=in_specs,
        out_specs=pl.BlockSpec((1, tok_rows, lanes), lambda j, off: (0, 0, j)),
    )
    return pl.pallas_call(
        functools.partial(attention_kernel, head_dim=head_dim),
        grid_spec=grid_spec,
        out_shape=jax.ShapeDtypeStruct(queries.shape, queries.dtype),
    )(offsets, *operands)


def level_features(levels, model_width):
    half_count = model_width // 2
    index_row = jnp.arange(half_count, dtype=jnp.float32)
    freqs = jnp.exp(-math.log(10000.0) * index_row / half_count)
    angles = levels.astype(jnp.float32)[:, None] * freqs[None, :]
    return jnp.concatenate([jnp.sin(angles), jnp.cos(angles)], axis=1)


def rms_norm(values):
    return values * lax.rsqrt(jnp.mean(values * values, axis=-1, keepdims=True) + 1e-06)


def condition(gathered, level_feat):
    return (rms_norm(gathered.astype(jnp.float32)) + level_feat[:, None, :]).astype(jnp.bfloat16)


def per_device(noisy, levels, pairs, w_qkv, w_out, w_up, w_down):
    level_feat = level_features(levels, D)
    w_out_other = other_w_out(w_out)
    outs = [
        one_sample(
            noisy[s:s + 1], level_feat[s:s + 1], pairs, w_qkv, w_out, w_out_other, w_up, w_down
        )
        for s in range(noisy.shape[0])
    ]
    return jnp.concatenate(outs, axis=0)


def one_sample(noisy, level_feat, pairs, w_qkv, w_out, w_out_other, w_up, w_down):
    samples, tok_rows, half_width = noisy.shape
    tp_index = lax.axis_index("tp")
    noisy_other = tp_swap(noisy)
    gathered = tp_join(noisy, noisy_other, tp_index)
    normed = condition(gathered, level_feat)
    projected = jnp.einsum(
        "std,cde->cste", normed, w_qkv, preferred_element_type=jnp.float32
    ).astype(jnp.bfloat16)
    queries, keys_here, values_here = (projected[0], projected[1], projected[2])
    blocks_dev = tok_rows // BLOCK
    head_dim = D // HEADS
    local_width = w_qkv.shape[2]
    local_heads = local_width // head_dim
    axis_bits = lax.axis_size("seq").bit_length() - 1
    kv_here = jnp.stack([keys_here, values_here])
    offsets = (pairs % blocks_dev).astype(jnp.int32).reshape(-1)
    got = []
    for section_idx in range(SECTIONS):
        bit_pos = axis_bits - 1 - section_idx
        got.append(
            partner(kv_here, "seq", bit_pos).reshape(2, samples, blocks_dev, BLOCK, local_width)
        )
    mixed = block_attention(queries, kv_here, got, offsets, local_heads, head_dim)
    mixed_other = tp_swap(mixed)
    attn = jnp.einsum("sth,hd->std", mixed, w_out, preferred_element_type=jnp.float32)
    attn = attn + jnp.einsum(
        "sth,hd->std", mixed_other, w_out_other, preferred_element_type=jnp.float32
    )
    middle = (gathered.astype(jnp.float32) + attn).astype(jnp.bfloat16)
    middle_half = tp_half(middle, tp_index, half_width)
    inner = rms_norm(middle.astype(jnp.float32)).astype(jnp.bfloat16)
    hidden = jax.nn.gelu(
        jnp.einsum("std,df->stf", inner, w_up, preferred_element_type=jnp.float32), approximate=True
    ).astype(jnp.bfloat16)
    down_part = jnp.einsum("stf,fd->std", hidden, w_down, preferred_element_type=jnp.float32)
    down_own = tp_half(down_part, tp_index, half_width)
    down_send = tp_half(down_part, 1 - tp_index, half_width).astype(jnp.bfloat16)
    down_half = down_own + tp_swap(down_send).astype(jnp.float32)
    return (middle_half.astype(jnp.float32) + down_half).astype(jnp.bfloat16)


def solution(mesh):
    in_specs = (
        P(None, "seq", "tp"),
        P(),
        P("seq", None),
        P(None, None, "tp"),
        P("tp", None),
        P(None, "tp"),
        P("tp", None),
    )
    out_specs = P(None, "seq", "tp")
    return jax.shard_map(
        per_device, mesh=mesh, in_specs=in_specs, out_specs=out_specs, check_vma=False
    )
```

```python
import functools
import math

import jax
import jax.numpy as jnp
from jax import lax
from jax.experimental import pallas as pl
from jax.experimental.pallas import tpu as pltpu
from jax.sharding import PartitionSpec as P


D = 1024
HEADS = 16
BLOCK = 128
SECTIONS = 4


def partner(x, axis, stride):
    return lax.ppermute(x, axis, [(i, i ^ 1 << stride) for i in range(lax.axis_size(axis))])


def tp_swap(x):
    return lax.ppermute(x, "tp", [(0, 1), (1, 0)])


def other_w_out(w_out):
    seq_size = lax.axis_size("seq")
    tp_size = lax.axis_size("tp")
    far = seq_size // 2
    perm = [
        (s * tp_size + t, (s ^ far) * tp_size + (tp_size - 1 - t))
        for s in range(seq_size)
        for t in range(tp_size)
    ]
    return lax.ppermute(w_out, ("seq", "tp"), perm)


def tp_join(own, other, tp_index):
    first = jnp.where(tp_index == 0, own, other)
    second = jnp.where(tp_index == 0, other, own)
    return jnp.concatenate([first, second], axis=-1)


def tp_half(x, index, width):
    return lax.dynamic_slice_in_dim(x, index * width, width, axis=x.ndim - 1)


def attention_kernel(off_ref, q_ref, kn_ref, vn_ref, *refs, head_dim):
    far_k = refs[0:2 * SECTIONS:2]
    far_v = refs[1:2 * SECTIONS:2]
    out_ref = refs[2 * SECTIONS]
    scale = 1.0 / math.sqrt(head_dim)
    dims = (((1,), (1,)), ((), ()))
    q = q_ref[0]
    tok_rows = q.shape[0]
    key_near = kn_ref[0, 0]
    value_near = vn_ref[0, 0]
    first = lax.broadcasted_iota(jnp.int32, q.shape, 1) < head_dim
    far_keys = []
    far_values = []
    for b in range(tok_rows // BLOCK):
        picks = [off_ref[b * SECTIONS + c] for c in range(SECTIONS)]
        far_keys.append(jnp.concatenate([far_k[c][0, 0, picks[c]] for c in range(SECTIONS)], axis=0))
        far_values.append(jnp.concatenate([far_v[c][0, 0, picks[c]] for c in range(SECTIONS)], axis=0))
    halves = []
    for own in (first, jnp.logical_not(first)):
        q_head = jnp.where(own, q, jnp.zeros_like(q))
        near_scores = lax.dot_general(q_head, key_near, dims, preferred_element_type=jnp.float32) * scale
        near_probs = []
        far_mixed = []
        for b in range(tok_rows // BLOCK):
            rows = slice(b * BLOCK, (b + 1) * BLOCK)
            near_b = near_scores[rows]
            far_b = lax.dot_general(
                q_head[rows], far_keys[b], dims, preferred_element_type=jnp.float32
            ) * scale
            top = jnp.maximum(near_b.max(axis=-1, keepdims=True), far_b.max(axis=-1, keepdims=True))
            near_e = jnp.exp(near_b - top)
            far_e = jnp.exp(far_b - top)
            total = near_e.sum(axis=-1, keepdims=True) + far_e.sum(axis=-1, keepdims=True)
            near_probs.append((near_e / total).astype(jnp.bfloat16))
            far_mixed.append(
                jnp.dot((far_e / total).astype(jnp.bfloat16), far_values[b],
                        preferred_element_type=jnp.float32)
            )
        mixed = jnp.dot(
            jnp.concatenate(near_probs, axis=0), value_near, preferred_element_type=jnp.float32
        ) + jnp.concatenate(far_mixed, axis=0)
        halves.append(mixed)
    out_ref[0] = jnp.where(first, halves[0], halves[1]).astype(out_ref.dtype)


def block_attention(queries, kv_here, got, offsets, head_dim):
    _, tok_rows, width = queries.shape
    blocks_dev = tok_rows // BLOCK
    lanes = 2 * head_dim
    in_specs = [
        pl.BlockSpec((1, tok_rows, lanes), lambda j, off: (0, 0, j)),
        pl.BlockSpec((1, 1, tok_rows, lanes), lambda j, off: (0, 0, 0, j)),
        pl.BlockSpec((1, 1, tok_rows, lanes), lambda j, off: (1, 0, 0, j)),
    ]
    operands = [queries, kv_here, kv_here]
    for section_idx in range(SECTIONS):
        for which in range(2):
            in_specs.append(
                pl.BlockSpec(
                    (1, 1, blocks_dev, BLOCK, lanes),
                    lambda j, off, w=which: (w, 0, 0, 0, j),
                )
            )
            operands.append(got[section_idx])
    grid_spec = pltpu.PrefetchScalarGridSpec(
        num_scalar_prefetch=1,
        grid=(width // lanes,),
        in_specs=in_specs,
        out_specs=pl.BlockSpec((1, tok_rows, lanes), lambda j, off: (0, 0, j)),
    )
    return pl.pallas_call(
        functools.partial(attention_kernel, head_dim=head_dim),
        grid_spec=grid_spec,
        out_shape=jax.ShapeDtypeStruct(queries.shape, queries.dtype),
    )(offsets, *operands)


def level_features(levels, model_width):
    half_count = model_width // 2
    index_row = jnp.arange(half_count, dtype=jnp.float32)
    freqs = jnp.exp(-math.log(10000.0) * index_row / half_count)
    angles = levels.astype(jnp.float32)[:, None] * freqs[None, :]
    return jnp.concatenate([jnp.sin(angles), jnp.cos(angles)], axis=1)


def rms_norm(values):
    return values * lax.rsqrt(jnp.mean(values * values, axis=-1, keepdims=True) + 1e-06)


def condition(gathered, level_feat):
    return (rms_norm(gathered.astype(jnp.float32)) + level_feat[:, None, :]).astype(jnp.bfloat16)


def per_device(noisy, levels, pairs, w_qkv, w_out, w_up, w_down):
    level_feat = level_features(levels, D)
    w_out_other = other_w_out(w_out)
    outs = []
    for s in range(noisy.shape[0]):
        outs.append(
            one_sample(
                noisy[s:s + 1], level_feat[s:s + 1], pairs, w_qkv, w_out, w_out_other,
                w_up, w_down,
            )
        )
    return jnp.concatenate(outs, axis=0)


def one_sample(noisy, level_feat, pairs, w_qkv, w_out, w_out_other, w_up, w_down):
    samples, tok_rows, half_width = noisy.shape
    tp_index = lax.axis_index("tp")
    noisy_other = tp_swap(noisy)
    gathered = tp_join(noisy, noisy_other, tp_index)
    normed = condition(gathered, level_feat)
    projected = jnp.einsum(
        "std,cde->cste", normed, w_qkv, preferred_element_type=jnp.float32
    ).astype(jnp.bfloat16)
    queries, keys_here, values_here = (projected[0], projected[1], projected[2])
    blocks_dev = tok_rows // BLOCK
    head_dim = D // HEADS
    local_width = w_qkv.shape[2]
    axis_bits = lax.axis_size("seq").bit_length() - 1
    kv_here = jnp.stack([keys_here, values_here])
    offsets = (pairs % blocks_dev).astype(jnp.int32).reshape(-1)
    got = [None] * SECTIONS
    for section_idx in reversed(range(SECTIONS)):
        bit_pos = axis_bits - 1 - section_idx
        got[section_idx] = partner(kv_here, "seq", bit_pos).reshape(
            2, samples, blocks_dev, BLOCK, local_width
        )
    mixed = block_attention(queries, kv_here, got, offsets, head_dim)
    mixed_other = tp_swap(mixed)
    attn = jnp.einsum("sth,hd->std", mixed, w_out, preferred_element_type=jnp.float32)
    attn = attn + jnp.einsum(
        "sth,hd->std", mixed_other, w_out_other, preferred_element_type=jnp.float32
    )
    middle = (gathered.astype(jnp.float32) + attn).astype(jnp.bfloat16)
    middle_half = tp_half(middle, tp_index, half_width)
    inner = rms_norm(middle.astype(jnp.float32)).astype(jnp.bfloat16)
    hidden = jax.nn.gelu(
        jnp.einsum("std,df->stf", inner, w_up, preferred_element_type=jnp.float32), approximate=True
    ).astype(jnp.bfloat16)
    down_part = jnp.einsum("stf,fd->std", hidden, w_down, preferred_element_type=jnp.float32)
    down_own = tp_half(down_part, tp_index, half_width)
    down_send = tp_half(down_part, 1 - tp_index, half_width).astype(jnp.bfloat16)
    down_half = down_own + tp_swap(down_send).astype(jnp.float32)
    return (middle_half.astype(jnp.float32) + down_half).astype(jnp.bfloat16)


def solution(mesh):
    in_specs = (
        P(None, "seq", "tp"),
        P(),
        P("seq", None),
        P(None, None, "tp"),
        P("tp", None),
        P(None, "tp"),
        P("tp", None),
    )
    out_specs = P(None, "seq", "tp")
    return jax.shard_map(
        per_device, mesh=mesh, in_specs=in_specs, out_specs=out_specs, check_vma=False
    )
```

```python
import functools
import math

import jax
import jax.numpy as jnp
from jax import lax
from jax.experimental import pallas as pl
from jax.experimental.pallas import tpu as pltpu
from jax.sharding import PartitionSpec as P


D = 1024
HEADS = 16
BLOCK = 128
SECTIONS = 4


def partner(x, axis, stride):
    return lax.ppermute(x, axis, [(i, i ^ 1 << stride) for i in range(lax.axis_size(axis))])


def tp_swap(x):
    return lax.ppermute(x, "tp", [(0, 1), (1, 0)])


def other_w_out(w_out):
    seq_size = lax.axis_size("seq")
    tp_size = lax.axis_size("tp")
    far = seq_size // 2
    perm = [
        (s * tp_size + t, (s ^ far) * tp_size + (tp_size - 1 - t))
        for s in range(seq_size)
        for t in range(tp_size)
    ]
    return lax.ppermute(w_out, ("seq", "tp"), perm)


def tp_join(own, other, tp_index):
    first = jnp.where(tp_index == 0, own, other)
    second = jnp.where(tp_index == 0, other, own)
    return jnp.concatenate([first, second], axis=-1)


def tp_half(x, index, width):
    return lax.dynamic_slice_in_dim(x, index * width, width, axis=x.ndim - 1)


def near_kernel(q_ref, kn_ref, vn_ref, o_ref, m_ref, l_ref, *, head_dim):
    scale = 1.0 / math.sqrt(head_dim)
    dims = (((1,), (1,)), ((), ()))
    q = q_ref[0]
    key_near = kn_ref[0, 0]
    value_near = vn_ref[0, 0]
    first = lax.broadcasted_iota(jnp.int32, q.shape, 1) < head_dim
    parts = []
    for own in (first, jnp.logical_not(first)):
        q_head = jnp.where(own, q, jnp.zeros_like(q))
        scores = lax.dot_general(q_head, key_near, dims, preferred_element_type=jnp.float32) * scale
        top = scores.max(axis=-1, keepdims=True)
        expd = jnp.exp(scores - top)
        total = expd.sum(axis=-1, keepdims=True)
        mixed = jnp.dot(expd.astype(jnp.bfloat16), value_near, preferred_element_type=jnp.float32)
        parts.append((mixed, top, total))
    o_ref[0] = jnp.where(first, parts[0][0], parts[1][0])
    m_ref[0] = jnp.where(first, parts[0][1], parts[1][1])
    l_ref[0] = jnp.where(first, parts[0][2], parts[1][2])


def far_kernel(off_ref, q_ref, on_ref, mn_ref, ln_ref, *refs, head_dim):
    far_k = refs[0:2 * SECTIONS:2]
    far_v = refs[1:2 * SECTIONS:2]
    out_ref = refs[2 * SECTIONS]
    scale = 1.0 / math.sqrt(head_dim)
    dims = (((1,), (1,)), ((), ()))
    q = q_ref[0]
    tok_rows = q.shape[0]
    first = lax.broadcasted_iota(jnp.int32, q.shape, 1) < head_dim
    far_keys = []
    far_values = []
    for b in range(tok_rows // BLOCK):
        picks = [off_ref[b * SECTIONS + c] for c in range(SECTIONS)]
        far_keys.append(jnp.concatenate([far_k[c][0, 0, picks[c]] for c in range(SECTIONS)], axis=0))
        far_values.append(jnp.concatenate([far_v[c][0, 0, picks[c]] for c in range(SECTIONS)], axis=0))
    parts = []
    for own in (first, jnp.logical_not(first)):
        q_head = jnp.where(own, q, jnp.zeros_like(q))
        mixed, tops, totals = [], [], []
        for b in range(tok_rows // BLOCK):
            rows = slice(b * BLOCK, (b + 1) * BLOCK)
            scores = lax.dot_general(
                q_head[rows], far_keys[b], dims, preferred_element_type=jnp.float32
            ) * scale
            top = scores.max(axis=-1, keepdims=True)
            expd = jnp.exp(scores - top)
            totals.append(expd.sum(axis=-1, keepdims=True))
            tops.append(top)
            mixed.append(
                jnp.dot(expd.astype(jnp.bfloat16), far_values[b], preferred_element_type=jnp.float32)
            )
        parts.append(
            (
                jnp.concatenate(mixed, axis=0),
                jnp.concatenate(tops, axis=0),
                jnp.concatenate(totals, axis=0),
            )
        )
    far_o = jnp.where(first, parts[0][0], parts[1][0])
    far_m = jnp.where(first, parts[0][1], parts[1][1])
    far_l = jnp.where(first, parts[0][2], parts[1][2])
    near_o = on_ref[0]
    near_m = mn_ref[0]
    near_l = ln_ref[0]
    top = jnp.maximum(near_m, far_m)
    near_w = jnp.exp(near_m - top)
    far_w = jnp.exp(far_m - top)
    mixed = (near_o * near_w + far_o * far_w) / (near_l * near_w + far_l * far_w)
    out_ref[0] = mixed.astype(out_ref.dtype)


def near_attention(queries, kv_here, head_dim):
    _, tok_rows, width = queries.shape
    lanes = 2 * head_dim
    row_spec = pl.BlockSpec((1, tok_rows, lanes), lambda j: (0, 0, j))
    stat = jax.ShapeDtypeStruct(queries.shape, jnp.float32)
    return pl.pallas_call(
        functools.partial(near_kernel, head_dim=head_dim),
        grid=(width // lanes,),
        in_specs=[
            row_spec,
            pl.BlockSpec((1, 1, tok_rows, lanes), lambda j: (0, 0, 0, j)),
            pl.BlockSpec((1, 1, tok_rows, lanes), lambda j: (1, 0, 0, j)),
        ],
        out_specs=[row_spec, row_spec, row_spec],
        out_shape=[stat, stat, stat],
    )(queries, kv_here, kv_here)


def far_attention(queries, near, got, offsets, head_dim):
    _, tok_rows, width = queries.shape
    blocks_dev = tok_rows // BLOCK
    lanes = 2 * head_dim
    row_spec = pl.BlockSpec((1, tok_rows, lanes), lambda j, off: (0, 0, j))
    in_specs = [row_spec, row_spec, row_spec, row_spec]
    operands = [queries, *near]
    for section_idx in range(SECTIONS):
        for which in range(2):
            in_specs.append(
                pl.BlockSpec(
                    (1, 1, blocks_dev, BLOCK, lanes),
                    lambda j, off, w=which: (w, 0, 0, 0, j),
                )
            )
            operands.append(got[section_idx])
    grid_spec = pltpu.PrefetchScalarGridSpec(
        num_scalar_prefetch=1,
        grid=(width // lanes,),
        in_specs=in_specs,
        out_specs=row_spec,
    )
    return pl.pallas_call(
        functools.partial(far_kernel, head_dim=head_dim),
        grid_spec=grid_spec,
        out_shape=jax.ShapeDtypeStruct(queries.shape, queries.dtype),
    )(offsets, *operands)


def level_features(levels, model_width):
    half_count = model_width // 2
    index_row = jnp.arange(half_count, dtype=jnp.float32)
    freqs = jnp.exp(-math.log(10000.0) * index_row / half_count)
    angles = levels.astype(jnp.float32)[:, None] * freqs[None, :]
    return jnp.concatenate([jnp.sin(angles), jnp.cos(angles)], axis=1)


def rms_norm(values):
    return values * lax.rsqrt(jnp.mean(values * values, axis=-1, keepdims=True) + 1e-06)


def condition(gathered, level_feat):
    return (rms_norm(gathered.astype(jnp.float32)) + level_feat[:, None, :]).astype(jnp.bfloat16)


def per_device(noisy, levels, pairs, w_qkv, w_out, w_up, w_down):
    level_feat = level_features(levels, D)
    w_out_other = other_w_out(w_out)
    outs = []
    for s in range(noisy.shape[0]):
        outs.append(
            one_sample(
                noisy[s:s + 1], level_feat[s:s + 1], pairs, w_qkv, w_out, w_out_other,
                w_up, w_down,
            )
        )
    return jnp.concatenate(outs, axis=0)


def one_sample(noisy, level_feat, pairs, w_qkv, w_out, w_out_other, w_up, w_down):
    samples, tok_rows, half_width = noisy.shape
    tp_index = lax.axis_index("tp")
    noisy_other = tp_swap(noisy)
    gathered = tp_join(noisy, noisy_other, tp_index)
    normed = condition(gathered, level_feat)
    projected = jnp.einsum(
        "std,cde->cste", normed, w_qkv, preferred_element_type=jnp.float32
    ).astype(jnp.bfloat16)
    queries, keys_here, values_here = (projected[0], projected[1], projected[2])
    blocks_dev = tok_rows // BLOCK
    head_dim = D // HEADS
    local_width = w_qkv.shape[2]
    axis_bits = lax.axis_size("seq").bit_length() - 1
    kv_here = jnp.stack([keys_here, values_here])
    offsets = (pairs % blocks_dev).astype(jnp.int32).reshape(-1)
    got = [None] * SECTIONS
    for section_idx in reversed(range(SECTIONS)):
        bit_pos = axis_bits - 1 - section_idx
        got[section_idx] = partner(kv_here, "seq", bit_pos).reshape(
            2, samples, blocks_dev, BLOCK, local_width
        )
    near = near_attention(queries, kv_here, head_dim)
    mixed = far_attention(queries, near, got, offsets, head_dim)
    mixed_other = tp_swap(mixed)
    attn = jnp.einsum("sth,hd->std", mixed, w_out, preferred_element_type=jnp.float32)
    attn = attn + jnp.einsum(
        "sth,hd->std", mixed_other, w_out_other, preferred_element_type=jnp.float32
    )
    middle = (gathered.astype(jnp.float32) + attn).astype(jnp.bfloat16)
    middle_half = tp_half(middle, tp_index, half_width)
    inner = rms_norm(middle.astype(jnp.float32)).astype(jnp.bfloat16)
    hidden = jax.nn.gelu(
        jnp.einsum("std,df->stf", inner, w_up, preferred_element_type=jnp.float32), approximate=True
    ).astype(jnp.bfloat16)
    down_part = jnp.einsum("stf,fd->std", hidden, w_down, preferred_element_type=jnp.float32)
    down_own = tp_half(down_part, tp_index, half_width)
    down_send = tp_half(down_part, 1 - tp_index, half_width).astype(jnp.bfloat16)
    down_half = down_own + tp_swap(down_send).astype(jnp.float32)
    return (middle_half.astype(jnp.float32) + down_half).astype(jnp.bfloat16)


def solution(mesh):
    in_specs = (
        P(None, "seq", "tp"),
        P(),
        P("seq", None),
        P(None, None, "tp"),
        P("tp", None),
        P(None, "tp"),
        P("tp", None),
    )
    out_specs = P(None, "seq", "tp")
    return jax.shard_map(
        per_device, mesh=mesh, in_specs=in_specs, out_specs=out_specs, check_vma=False
    )
```

```python
import functools
import math

import jax
import jax.numpy as jnp
from jax import lax
from jax.experimental import pallas as pl
from jax.experimental.pallas import tpu as pltpu
from jax.sharding import PartitionSpec as P


D = 1024
HEADS = 16
BLOCK = 128
SECTIONS = 4


def partner(x, axis, stride):
    return lax.ppermute(x, axis, [(i, i ^ 1 << stride) for i in range(lax.axis_size(axis))])


def tp_swap(x):
    return lax.ppermute(x, "tp", [(0, 1), (1, 0)])


def other_w_out(w_out):
    seq_size = lax.axis_size("seq")
    tp_size = lax.axis_size("tp")
    far = seq_size // 2
    perm = [
        (s * tp_size + t, (s ^ far) * tp_size + (tp_size - 1 - t))
        for s in range(seq_size)
        for t in range(tp_size)
    ]
    return lax.ppermute(w_out, ("seq", "tp"), perm)


def tp_join(own, other, tp_index):
    first = jnp.where(tp_index == 0, own, other)
    second = jnp.where(tp_index == 0, other, own)
    return jnp.concatenate([first, second], axis=-1)


def tp_half(x, index, width):
    return lax.dynamic_slice_in_dim(x, index * width, width, axis=x.ndim - 1)


def near_kernel(q_ref, kn_ref, vn_ref, o_ref, m_ref, l_ref, *, head_dim):
    scale = 1.0 / math.sqrt(head_dim)
    dims = (((1,), (1,)), ((), ()))
    q = q_ref[0]
    key_near = kn_ref[0, 0]
    value_near = vn_ref[0, 0]
    first = lax.broadcasted_iota(jnp.int32, q.shape, 1) < head_dim
    parts = []
    for own in (first, jnp.logical_not(first)):
        q_head = jnp.where(own, q, jnp.zeros_like(q))
        scores = lax.dot_general(q_head, key_near, dims, preferred_element_type=jnp.float32) * scale
        top = scores.max(axis=-1, keepdims=True)
        expd = jnp.exp(scores - top)
        total = expd.sum(axis=-1, keepdims=True)
        mixed = jnp.dot(expd.astype(jnp.bfloat16), value_near, preferred_element_type=jnp.float32)
        parts.append((mixed, top, total))
    o_ref[0] = jnp.where(first, parts[0][0], parts[1][0])
    m_ref[0] = jnp.where(first, parts[0][1], parts[1][1])
    l_ref[0] = jnp.where(first, parts[0][2], parts[1][2])


def far_kernel(off_ref, q_ref, on_ref, mn_ref, ln_ref, *refs, head_dim):
    far_k = refs[0:2 * SECTIONS:2]
    far_v = refs[1:2 * SECTIONS:2]
    out_ref = refs[2 * SECTIONS]
    scale = 1.0 / math.sqrt(head_dim)
    dims = (((1,), (1,)), ((), ()))
    q = q_ref[0]
    tok_rows = q.shape[0]
    first = lax.broadcasted_iota(jnp.int32, q.shape, 1) < head_dim
    far_keys = []
    far_values = []
    for b in range(tok_rows // BLOCK):
        picks = [off_ref[b * SECTIONS + c] for c in range(SECTIONS)]
        far_keys.append(jnp.concatenate([far_k[c][0, 0, picks[c]] for c in range(SECTIONS)], axis=0))
        far_values.append(jnp.concatenate([far_v[c][0, 0, picks[c]] for c in range(SECTIONS)], axis=0))
    parts = []
    for own in (first, jnp.logical_not(first)):
        q_head = jnp.where(own, q, jnp.zeros_like(q))
        mixed, tops, totals = [], [], []
        for b in range(tok_rows // BLOCK):
            rows = slice(b * BLOCK, (b + 1) * BLOCK)
            scores = lax.dot_general(
                q_head[rows], far_keys[b], dims, preferred_element_type=jnp.float32
            ) * scale
            top = scores.max(axis=-1, keepdims=True)
            expd = jnp.exp(scores - top)
            totals.append(expd.sum(axis=-1, keepdims=True))
            tops.append(top)
            mixed.append(
                jnp.dot(expd.astype(jnp.bfloat16), far_values[b], preferred_element_type=jnp.float32)
            )
        parts.append(
            (
                jnp.concatenate(mixed, axis=0),
                jnp.concatenate(tops, axis=0),
                jnp.concatenate(totals, axis=0),
            )
        )
    far_o = jnp.where(first, parts[0][0], parts[1][0])
    far_m = jnp.where(first, parts[0][1], parts[1][1])
    far_l = jnp.where(first, parts[0][2], parts[1][2])
    near_o = on_ref[0]
    near_m = mn_ref[0]
    near_l = ln_ref[0]
    top = jnp.maximum(near_m, far_m)
    near_w = jnp.exp(near_m - top)
    far_w = jnp.exp(far_m - top)
    mixed = (near_o * near_w + far_o * far_w) / (near_l * near_w + far_l * far_w)
    out_ref[0] = mixed.astype(out_ref.dtype)


def near_attention(queries, kv_here, head_dim):
    _, tok_rows, width = queries.shape
    lanes = 2 * head_dim
    row_spec = pl.BlockSpec((1, tok_rows, lanes), lambda j: (0, 0, j))
    stat = jax.ShapeDtypeStruct(queries.shape, jnp.float32)
    return pl.pallas_call(
        functools.partial(near_kernel, head_dim=head_dim),
        grid=(width // lanes,),
        in_specs=[
            row_spec,
            pl.BlockSpec((1, 1, tok_rows, lanes), lambda j: (0, 0, 0, j)),
            pl.BlockSpec((1, 1, tok_rows, lanes), lambda j: (1, 0, 0, j)),
        ],
        out_specs=[row_spec, row_spec, row_spec],
        out_shape=[stat, stat, stat],
    )(queries, kv_here, kv_here)


def far_attention(queries, near, got, offsets, head_dim):
    _, tok_rows, width = queries.shape
    blocks_dev = tok_rows // BLOCK
    lanes = 2 * head_dim
    row_spec = pl.BlockSpec((1, tok_rows, lanes), lambda j, off: (0, 0, j))
    in_specs = [row_spec, row_spec, row_spec, row_spec]
    operands = [queries, *near]
    for section_idx in range(SECTIONS):
        for which in range(2):
            in_specs.append(
                pl.BlockSpec(
                    (1, 1, blocks_dev, BLOCK, lanes),
                    lambda j, off, w=which: (w, 0, 0, 0, j),
                )
            )
            operands.append(got[section_idx])
    grid_spec = pltpu.PrefetchScalarGridSpec(
        num_scalar_prefetch=1,
        grid=(width // lanes,),
        in_specs=in_specs,
        out_specs=row_spec,
    )
    return pl.pallas_call(
        functools.partial(far_kernel, head_dim=head_dim),
        grid_spec=grid_spec,
        out_shape=jax.ShapeDtypeStruct(queries.shape, queries.dtype),
    )(offsets, *operands)


def level_features(levels, model_width):
    half_count = model_width // 2
    index_row = jnp.arange(half_count, dtype=jnp.float32)
    freqs = jnp.exp(-math.log(10000.0) * index_row / half_count)
    angles = levels.astype(jnp.float32)[:, None] * freqs[None, :]
    return jnp.concatenate([jnp.sin(angles), jnp.cos(angles)], axis=1)


def rms_norm(values):
    return values * lax.rsqrt(jnp.mean(values * values, axis=-1, keepdims=True) + 1e-06)


def condition(gathered, level_feat):
    return (rms_norm(gathered.astype(jnp.float32)) + level_feat[:, None, :]).astype(jnp.bfloat16)


def per_device(noisy, levels, pairs, w_qkv, w_out, w_up, w_down):
    level_feat = level_features(levels, D)
    w_out_other = other_w_out(w_out)
    tp_index = lax.axis_index("tp")
    half_width = noisy.shape[2]
    w_down = (tp_half(w_down, 1 - tp_index, half_width), tp_half(w_down, tp_index, half_width))
    outs = []
    for s in range(noisy.shape[0]):
        outs.append(
            one_sample(
                noisy[s:s + 1], level_feat[s:s + 1], pairs, w_qkv, w_out, w_out_other,
                w_up, w_down,
            )
        )
    return jnp.concatenate(outs, axis=0)


def one_sample(noisy, level_feat, pairs, w_qkv, w_out, w_out_other, w_up, w_down):
    samples, tok_rows, half_width = noisy.shape
    tp_index = lax.axis_index("tp")
    noisy_other = tp_swap(noisy)
    gathered = tp_join(noisy, noisy_other, tp_index)
    normed = condition(gathered, level_feat)
    projected = jnp.einsum(
        "std,cde->cste", normed, w_qkv, preferred_element_type=jnp.float32
    ).astype(jnp.bfloat16)
    queries, keys_here, values_here = (projected[0], projected[1], projected[2])
    blocks_dev = tok_rows // BLOCK
    head_dim = D // HEADS
    local_width = w_qkv.shape[2]
    axis_bits = lax.axis_size("seq").bit_length() - 1
    kv_here = jnp.stack([keys_here, values_here])
    offsets = (pairs % blocks_dev).astype(jnp.int32).reshape(-1)
    got = [None] * SECTIONS
    for section_idx in reversed(range(SECTIONS)):
        bit_pos = axis_bits - 1 - section_idx
        got[section_idx] = partner(kv_here, "seq", bit_pos).reshape(
            2, samples, blocks_dev, BLOCK, local_width
        )
    near = near_attention(queries, kv_here, head_dim)
    mixed = far_attention(queries, near, got, offsets, head_dim)
    mixed_other = tp_swap(mixed)
    attn = jnp.einsum("sth,hd->std", mixed, w_out, preferred_element_type=jnp.float32)
    attn = attn + jnp.einsum(
        "sth,hd->std", mixed_other, w_out_other, preferred_element_type=jnp.float32
    )
    middle = (gathered.astype(jnp.float32) + attn).astype(jnp.bfloat16)
    middle_half = tp_half(middle, tp_index, half_width)
    inner = rms_norm(middle.astype(jnp.float32)).astype(jnp.bfloat16)
    hidden = jax.nn.gelu(
        jnp.einsum("std,df->stf", inner, w_up, preferred_element_type=jnp.float32), approximate=True
    ).astype(jnp.bfloat16)
    w_down_send, w_down_own = w_down
    down_send = jnp.einsum(
        "stf,fd->std", hidden, w_down_send, preferred_element_type=jnp.float32
    ).astype(jnp.bfloat16)
    down_received = tp_swap(down_send)
    down_own = jnp.einsum("stf,fd->std", hidden, w_down_own, preferred_element_type=jnp.float32)
    down_half = down_own + down_received.astype(jnp.float32)
    return (middle_half.astype(jnp.float32) + down_half).astype(jnp.bfloat16)


def solution(mesh):
    in_specs = (
        P(None, "seq", "tp"),
        P(),
        P("seq", None),
        P(None, None, "tp"),
        P("tp", None),
        P(None, "tp"),
        P("tp", None),
    )
    out_specs = P(None, "seq", "tp")
    return jax.shard_map(
        per_device, mesh=mesh, in_specs=in_specs, out_specs=out_specs, check_vma=False
    )
```

```python
import functools
import math

import jax
import jax.numpy as jnp
from jax import lax
from jax.experimental import pallas as pl
from jax.experimental.pallas import tpu as pltpu
from jax.sharding import PartitionSpec as P


D = 1024
HEADS = 16
BLOCK = 128
SECTIONS = 4


def partner(x, axis, stride):
    return lax.ppermute(x, axis, [(i, i ^ 1 << stride) for i in range(lax.axis_size(axis))])


def tp_swap(x):
    return lax.ppermute(x, "tp", [(0, 1), (1, 0)])


def other_w_out(w_out):
    seq_size = lax.axis_size("seq")
    tp_size = lax.axis_size("tp")
    far = seq_size // 2
    perm = [
        (s * tp_size + t, (s ^ far) * tp_size + (tp_size - 1 - t))
        for s in range(seq_size)
        for t in range(tp_size)
    ]
    return lax.ppermute(w_out, ("seq", "tp"), perm)


def tp_join(own, other, tp_index):
    first = jnp.where(tp_index == 0, own, other)
    second = jnp.where(tp_index == 0, other, own)
    return jnp.concatenate([first, second], axis=-1)


def tp_half(x, index, width):
    return lax.dynamic_slice_in_dim(x, index * width, width, axis=x.ndim - 1)


def near_kernel(q_ref, kn_ref, vn_ref, o_ref, m_ref, l_ref, *, head_dim):
    scale = 1.0 / math.sqrt(head_dim)
    dims = (((1,), (1,)), ((), ()))
    q = q_ref[0]
    key_near = kn_ref[0, 0]
    value_near = vn_ref[0, 0]
    first = lax.broadcasted_iota(jnp.int32, q.shape, 1) < head_dim
    parts = []
    for own in (first, jnp.logical_not(first)):
        q_head = jnp.where(own, q, jnp.zeros_like(q))
        scores = lax.dot_general(q_head, key_near, dims, preferred_element_type=jnp.float32) * scale
        top = scores.max(axis=-1, keepdims=True)
        expd = jnp.exp(scores - top)
        total = expd.sum(axis=-1, keepdims=True)
        mixed = jnp.dot(expd.astype(jnp.bfloat16), value_near, preferred_element_type=jnp.float32)
        parts.append((mixed, top, total))
    o_ref[0] = jnp.where(first, parts[0][0], parts[1][0]).astype(o_ref.dtype)
    m_ref[0] = jnp.where(first, parts[0][1], parts[1][1])
    l_ref[0] = jnp.where(first, parts[0][2], parts[1][2])


def far_kernel(off_ref, q_ref, on_ref, mn_ref, ln_ref, *refs, head_dim):
    far_k = refs[0:2 * SECTIONS:2]
    far_v = refs[1:2 * SECTIONS:2]
    out_ref = refs[2 * SECTIONS]
    scale = 1.0 / math.sqrt(head_dim)
    dims = (((1,), (1,)), ((), ()))
    q = q_ref[0]
    tok_rows = q.shape[0]
    first = lax.broadcasted_iota(jnp.int32, q.shape, 1) < head_dim
    far_keys = []
    far_values = []
    for b in range(tok_rows // BLOCK):
        picks = [off_ref[b * SECTIONS + c] for c in range(SECTIONS)]
        far_keys.append(jnp.concatenate([far_k[c][0, 0, picks[c]] for c in range(SECTIONS)], axis=0))
        far_values.append(jnp.concatenate([far_v[c][0, 0, picks[c]] for c in range(SECTIONS)], axis=0))
    parts = []
    for own in (first, jnp.logical_not(first)):
        q_head = jnp.where(own, q, jnp.zeros_like(q))
        mixed, tops, totals = [], [], []
        for b in range(tok_rows // BLOCK):
            rows = slice(b * BLOCK, (b + 1) * BLOCK)
            scores = lax.dot_general(
                q_head[rows], far_keys[b], dims, preferred_element_type=jnp.float32
            ) * scale
            top = scores.max(axis=-1, keepdims=True)
            expd = jnp.exp(scores - top)
            totals.append(expd.sum(axis=-1, keepdims=True))
            tops.append(top)
            mixed.append(
                jnp.dot(expd.astype(jnp.bfloat16), far_values[b], preferred_element_type=jnp.float32)
            )
        parts.append(
            (
                jnp.concatenate(mixed, axis=0),
                jnp.concatenate(tops, axis=0),
                jnp.concatenate(totals, axis=0),
            )
        )
    far_o = jnp.where(first, parts[0][0], parts[1][0])
    far_m = jnp.where(first, parts[0][1], parts[1][1])
    far_l = jnp.where(first, parts[0][2], parts[1][2])
    near_o = on_ref[0].astype(jnp.float32)
    near_m = mn_ref[0]
    near_l = ln_ref[0]
    top = jnp.maximum(near_m, far_m)
    near_w = jnp.exp(near_m - top)
    far_w = jnp.exp(far_m - top)
    mixed = (near_o * near_w + far_o * far_w) / (near_l * near_w + far_l * far_w)
    out_ref[0] = mixed.astype(out_ref.dtype)


def near_attention(queries, kv_here, head_dim):
    _, tok_rows, width = queries.shape
    lanes = 2 * head_dim
    row_spec = pl.BlockSpec((1, tok_rows, lanes), lambda j: (0, 0, j))
    stat = jax.ShapeDtypeStruct(queries.shape, jnp.float32)
    part = jax.ShapeDtypeStruct(queries.shape, jnp.bfloat16)
    return pl.pallas_call(
        functools.partial(near_kernel, head_dim=head_dim),
        grid=(width // lanes,),
        in_specs=[
            row_spec,
            pl.BlockSpec((1, 1, tok_rows, lanes), lambda j: (0, 0, 0, j)),
            pl.BlockSpec((1, 1, tok_rows, lanes), lambda j: (1, 0, 0, j)),
        ],
        out_specs=[row_spec, row_spec, row_spec],
        out_shape=[part, stat, stat],
    )(queries, kv_here, kv_here)


def far_attention(queries, near, got, offsets, head_dim):
    _, tok_rows, width = queries.shape
    blocks_dev = tok_rows // BLOCK
    lanes = 2 * head_dim
    row_spec = pl.BlockSpec((1, tok_rows, lanes), lambda j, off: (0, 0, j))
    in_specs = [row_spec, row_spec, row_spec, row_spec]
    operands = [queries, *near]
    for section_idx in range(SECTIONS):
        for which in range(2):
            in_specs.append(
                pl.BlockSpec(
                    (1, 1, blocks_dev, BLOCK, lanes),
                    lambda j, off, w=which: (w, 0, 0, 0, j),
                )
            )
            operands.append(got[section_idx])
    grid_spec = pltpu.PrefetchScalarGridSpec(
        num_scalar_prefetch=1,
        grid=(width // lanes,),
        in_specs=in_specs,
        out_specs=row_spec,
    )
    return pl.pallas_call(
        functools.partial(far_kernel, head_dim=head_dim),
        grid_spec=grid_spec,
        out_shape=jax.ShapeDtypeStruct(queries.shape, queries.dtype),
    )(offsets, *operands)


def level_features(levels, model_width):
    half_count = model_width // 2
    index_row = jnp.arange(half_count, dtype=jnp.float32)
    freqs = jnp.exp(-math.log(10000.0) * index_row / half_count)
    angles = levels.astype(jnp.float32)[:, None] * freqs[None, :]
    return jnp.concatenate([jnp.sin(angles), jnp.cos(angles)], axis=1)


def rms_norm(values):
    return values * lax.rsqrt(jnp.mean(values * values, axis=-1, keepdims=True) + 1e-06)


def condition(gathered, level_feat):
    return (rms_norm(gathered.astype(jnp.float32)) + level_feat[:, None, :]).astype(jnp.bfloat16)


def per_device(noisy, levels, pairs, w_qkv, w_out, w_up, w_down):
    level_feat = level_features(levels, D)
    w_out_other = other_w_out(w_out)
    tp_index = lax.axis_index("tp")
    half_width = noisy.shape[2]
    w_down = (tp_half(w_down, 1 - tp_index, half_width), tp_half(w_down, tp_index, half_width))
    outs = []
    for s in range(noisy.shape[0]):
        outs.append(
            one_sample(
                noisy[s:s + 1], level_feat[s:s + 1], pairs, w_qkv, w_out, w_out_other,
                w_up, w_down,
            )
        )
    return jnp.concatenate(outs, axis=0)


def one_sample(noisy, level_feat, pairs, w_qkv, w_out, w_out_other, w_up, w_down):
    samples, tok_rows, half_width = noisy.shape
    tp_index = lax.axis_index("tp")
    noisy_other = tp_swap(noisy)
    gathered = tp_join(noisy, noisy_other, tp_index)
    normed = condition(gathered, level_feat)
    projected = jnp.einsum(
        "std,cde->cste", normed, w_qkv, preferred_element_type=jnp.float32
    ).astype(jnp.bfloat16)
    queries, keys_here, values_here = (projected[0], projected[1], projected[2])
    blocks_dev = tok_rows // BLOCK
    head_dim = D // HEADS
    local_width = w_qkv.shape[2]
    axis_bits = lax.axis_size("seq").bit_length() - 1
    kv_here = jnp.stack([keys_here, values_here])
    offsets = (pairs % blocks_dev).astype(jnp.int32).reshape(-1)
    got = [None] * SECTIONS
    for section_idx in reversed(range(SECTIONS)):
        bit_pos = axis_bits - 1 - section_idx
        got[section_idx] = partner(kv_here, "seq", bit_pos).reshape(
            2, samples, blocks_dev, BLOCK, local_width
        )
    near = near_attention(queries, kv_here, head_dim)
    mixed = far_attention(queries, near, got, offsets, head_dim)
    mixed_other = tp_swap(mixed)
    attn = jnp.einsum("sth,hd->std", mixed, w_out, preferred_element_type=jnp.float32)
    attn = attn + jnp.einsum(
        "sth,hd->std", mixed_other, w_out_other, preferred_element_type=jnp.float32
    )
    middle = (gathered.astype(jnp.float32) + attn).astype(jnp.bfloat16)
    middle_half = tp_half(middle, tp_index, half_width)
    inner = rms_norm(middle.astype(jnp.float32)).astype(jnp.bfloat16)
    hidden = jax.nn.gelu(
        jnp.einsum("std,df->stf", inner, w_up, preferred_element_type=jnp.float32), approximate=True
    ).astype(jnp.bfloat16)
    w_down_send, w_down_own = w_down
    down_send = jnp.einsum(
        "stf,fd->std", hidden, w_down_send, preferred_element_type=jnp.float32
    ).astype(jnp.bfloat16)
    down_received = tp_swap(down_send)
    down_own = jnp.einsum("stf,fd->std", hidden, w_down_own, preferred_element_type=jnp.float32)
    down_half = down_own + down_received.astype(jnp.float32)
    return (middle_half.astype(jnp.float32) + down_half).astype(jnp.bfloat16)


def solution(mesh):
    in_specs = (
        P(None, "seq", "tp"),
        P(),
        P("seq", None),
        P(None, None, "tp"),
        P("tp", None),
        P(None, "tp"),
        P("tp", None),
    )
    out_specs = P(None, "seq", "tp")
    return jax.shard_map(
        per_device, mesh=mesh, in_specs=in_specs, out_specs=out_specs, check_vma=False
    )
```

```python
import functools
import math

import jax
import jax.numpy as jnp
from jax import lax
from jax.experimental import pallas as pl
from jax.experimental.pallas import tpu as pltpu
from jax.sharding import PartitionSpec as P


D = 1024
HEADS = 16
BLOCK = 128
SECTIONS = 4


def partner(x, axis, stride):
    return lax.ppermute(x, axis, [(i, i ^ 1 << stride) for i in range(lax.axis_size(axis))])


def tp_swap(x):
    return lax.ppermute(x, "tp", [(0, 1), (1, 0)])


def other_w_out(w_out):
    seq_size = lax.axis_size("seq")
    tp_size = lax.axis_size("tp")
    far = seq_size // 2
    perm = [
        (s * tp_size + t, (s ^ far) * tp_size + (tp_size - 1 - t))
        for s in range(seq_size)
        for t in range(tp_size)
    ]
    return lax.ppermute(w_out, ("seq", "tp"), perm)


def tp_half(x, index, width):
    return lax.dynamic_slice_in_dim(x, index * width, width, axis=x.ndim - 1)


def near_kernel(q_ref, kn_ref, vn_ref, o_ref, m_ref, l_ref, *, head_dim):
    scale = 1.0 / math.sqrt(head_dim)
    dims = (((1,), (1,)), ((), ()))
    q = q_ref[0]
    key_near = kn_ref[0, 0]
    value_near = vn_ref[0, 0]
    first = lax.broadcasted_iota(jnp.int32, q.shape, 1) < head_dim
    parts = []
    for own in (first, jnp.logical_not(first)):
        q_head = jnp.where(own, q, jnp.zeros_like(q))
        scores = lax.dot_general(q_head, key_near, dims, preferred_element_type=jnp.float32) * scale
        top = scores.max(axis=-1, keepdims=True)
        expd = jnp.exp(scores - top)
        total = expd.sum(axis=-1, keepdims=True)
        mixed = jnp.dot(expd.astype(jnp.bfloat16), value_near, preferred_element_type=jnp.float32)
        parts.append((mixed, top, total))
    o_ref[0] = jnp.where(first, parts[0][0], parts[1][0]).astype(o_ref.dtype)
    m_ref[0] = jnp.where(first, parts[0][1], parts[1][1])
    l_ref[0] = jnp.where(first, parts[0][2], parts[1][2])


def far_kernel(off_ref, q_ref, on_ref, mn_ref, ln_ref, *refs, head_dim):
    far_k = refs[0:2 * SECTIONS:2]
    far_v = refs[1:2 * SECTIONS:2]
    out_ref = refs[2 * SECTIONS]
    scale = 1.0 / math.sqrt(head_dim)
    dims = (((1,), (1,)), ((), ()))
    q = q_ref[0]
    tok_rows = q.shape[0]
    first = lax.broadcasted_iota(jnp.int32, q.shape, 1) < head_dim
    far_keys = []
    far_values = []
    for b in range(tok_rows // BLOCK):
        picks = [off_ref[b * SECTIONS + c] for c in range(SECTIONS)]
        far_keys.append(jnp.concatenate([far_k[c][0, 0, picks[c]] for c in range(SECTIONS)], axis=0))
        far_values.append(jnp.concatenate([far_v[c][0, 0, picks[c]] for c in range(SECTIONS)], axis=0))
    parts = []
    for own in (first, jnp.logical_not(first)):
        q_head = jnp.where(own, q, jnp.zeros_like(q))
        mixed, tops, totals = [], [], []
        for b in range(tok_rows // BLOCK):
            rows = slice(b * BLOCK, (b + 1) * BLOCK)
            scores = lax.dot_general(
                q_head[rows], far_keys[b], dims, preferred_element_type=jnp.float32
            ) * scale
            top = scores.max(axis=-1, keepdims=True)
            expd = jnp.exp(scores - top)
            totals.append(expd.sum(axis=-1, keepdims=True))
            tops.append(top)
            mixed.append(
                jnp.dot(expd.astype(jnp.bfloat16), far_values[b], preferred_element_type=jnp.float32)
            )
        parts.append(
            (
                jnp.concatenate(mixed, axis=0),
                jnp.concatenate(tops, axis=0),
                jnp.concatenate(totals, axis=0),
            )
        )
    far_o = jnp.where(first, parts[0][0], parts[1][0])
    far_m = jnp.where(first, parts[0][1], parts[1][1])
    far_l = jnp.where(first, parts[0][2], parts[1][2])
    near_o = on_ref[0].astype(jnp.float32)
    near_m = mn_ref[0]
    near_l = ln_ref[0]
    top = jnp.maximum(near_m, far_m)
    near_w = jnp.exp(near_m - top)
    far_w = jnp.exp(far_m - top)
    mixed = (near_o * near_w + far_o * far_w) / (near_l * near_w + far_l * far_w)
    out_ref[0] = mixed.astype(out_ref.dtype)


def near_attention(queries, kv_here, head_dim):
    _, tok_rows, width = queries.shape
    lanes = 2 * head_dim
    row_spec = pl.BlockSpec((1, tok_rows, lanes), lambda j: (0, 0, j))
    stat = jax.ShapeDtypeStruct(queries.shape, jnp.float32)
    part = jax.ShapeDtypeStruct(queries.shape, jnp.bfloat16)
    return pl.pallas_call(
        functools.partial(near_kernel, head_dim=head_dim),
        grid=(width // lanes,),
        in_specs=[
            row_spec,
            pl.BlockSpec((1, 1, tok_rows, lanes), lambda j: (0, 0, 0, j)),
            pl.BlockSpec((1, 1, tok_rows, lanes), lambda j: (1, 0, 0, j)),
        ],
        out_specs=[row_spec, row_spec, row_spec],
        out_shape=[part, stat, stat],
    )(queries, kv_here, kv_here)


def far_attention(queries, near, got, offsets, head_dim):
    _, tok_rows, width = queries.shape
    blocks_dev = tok_rows // BLOCK
    lanes = 2 * head_dim
    row_spec = pl.BlockSpec((1, tok_rows, lanes), lambda j, off: (0, 0, j))
    in_specs = [row_spec, row_spec, row_spec, row_spec]
    operands = [queries, *near]
    for section_idx in range(SECTIONS):
        for which in range(2):
            in_specs.append(
                pl.BlockSpec(
                    (1, 1, blocks_dev, BLOCK, lanes),
                    lambda j, off, w=which: (w, 0, 0, 0, j),
                )
            )
            operands.append(got[section_idx])
    grid_spec = pltpu.PrefetchScalarGridSpec(
        num_scalar_prefetch=1,
        grid=(width // lanes,),
        in_specs=in_specs,
        out_specs=row_spec,
    )
    return pl.pallas_call(
        functools.partial(far_kernel, head_dim=head_dim),
        grid_spec=grid_spec,
        out_shape=jax.ShapeDtypeStruct(queries.shape, queries.dtype),
    )(offsets, *operands)


def level_features(levels, model_width):
    half_count = model_width // 2
    index_row = jnp.arange(half_count, dtype=jnp.float32)
    freqs = jnp.exp(-math.log(10000.0) * index_row / half_count)
    angles = levels.astype(jnp.float32)[:, None] * freqs[None, :]
    return jnp.concatenate([jnp.sin(angles), jnp.cos(angles)], axis=1)


def rms_norm(values):
    return values * lax.rsqrt(jnp.mean(values * values, axis=-1, keepdims=True) + 1e-06)


def condition(gathered, level_feat):
    return (rms_norm(gathered.astype(jnp.float32)) + level_feat[:, None, :]).astype(jnp.bfloat16)


def per_device(noisy, levels, pairs, w_qkv, w_out, w_up, w_down):
    level_feat = level_features(levels, D)
    w_out_other = other_w_out(w_out)
    tp_index = lax.axis_index("tp")
    half_width = noisy.shape[2]
    w_down = (tp_half(w_down, 1 - tp_index, half_width), tp_half(w_down, tp_index, half_width))
    outs = []
    for s in range(noisy.shape[0]):
        outs.append(
            one_sample(
                noisy[s:s + 1], level_feat[s:s + 1], pairs, w_qkv, w_out, w_out_other,
                w_up, w_down,
            )
        )
    return jnp.concatenate(outs, axis=0)


def one_sample(noisy, level_feat, pairs, w_qkv, w_out, w_out_other, w_up, w_down):
    samples, tok_rows, half_width = noisy.shape
    tp_index = lax.axis_index("tp")
    noisy_other = tp_swap(noisy)
    gathered = lax.dynamic_update_slice_in_dim(
        jnp.concatenate([noisy_other, noisy_other], axis=-1), noisy, tp_index * half_width, axis=2
    )
    normed = condition(gathered, level_feat)
    projected = jnp.einsum(
        "std,cde->cste", normed, w_qkv, preferred_element_type=jnp.float32
    ).astype(jnp.bfloat16)
    queries, keys_here, values_here = (projected[0], projected[1], projected[2])
    blocks_dev = tok_rows // BLOCK
    head_dim = D // HEADS
    local_width = w_qkv.shape[2]
    axis_bits = lax.axis_size("seq").bit_length() - 1
    kv_here = jnp.stack([keys_here, values_here])
    offsets = (pairs % blocks_dev).astype(jnp.int32).reshape(-1)
    got = [None] * SECTIONS
    for section_idx in reversed(range(SECTIONS)):
        bit_pos = axis_bits - 1 - section_idx
        got[section_idx] = partner(kv_here, "seq", bit_pos).reshape(
            2, samples, blocks_dev, BLOCK, local_width
        )
    near = near_attention(queries, kv_here, head_dim)
    mixed = far_attention(queries, near, got, offsets, head_dim)
    mixed_other = tp_swap(mixed)
    attn = jnp.einsum("sth,hd->std", mixed, w_out, preferred_element_type=jnp.float32)
    attn = attn + jnp.einsum(
        "sth,hd->std", mixed_other, w_out_other, preferred_element_type=jnp.float32
    )
    middle = (gathered.astype(jnp.float32) + attn).astype(jnp.bfloat16)
    middle_half = tp_half(middle, tp_index, half_width)
    inner = rms_norm(middle.astype(jnp.float32)).astype(jnp.bfloat16)
    hidden = jax.nn.gelu(
        jnp.einsum("std,df->stf", inner, w_up, preferred_element_type=jnp.float32), approximate=True
    ).astype(jnp.bfloat16)
    w_down_send, w_down_own = w_down
    down_send = jnp.einsum(
        "stf,fd->std", hidden, w_down_send, preferred_element_type=jnp.float32
    ).astype(jnp.bfloat16)
    down_received = tp_swap(down_send)
    down_own = jnp.einsum("stf,fd->std", hidden, w_down_own, preferred_element_type=jnp.float32)
    down_half = down_own + down_received.astype(jnp.float32)
    return (middle_half.astype(jnp.float32) + down_half).astype(jnp.bfloat16)


def solution(mesh):
    in_specs = (
        P(None, "seq", "tp"),
        P(),
        P("seq", None),
        P(None, None, "tp"),
        P("tp", None),
        P(None, "tp"),
        P("tp", None),
    )
    out_specs = P(None, "seq", "tp")
    return jax.shard_map(
        per_device, mesh=mesh, in_specs=in_specs, out_specs=out_specs, check_vma=False
    )
```
